128 devices in a mesh: elem: 32 (over y, z, core), sub: 4 (over x).
Axes of the slice: x: 4, y: 4, z: 4, core: 2. Of those that a mesh axis runs over, the one named last changes fastest.
Arguments:
- tracers: bfloat16 [1024, 128, 1024], P('elem', 'sub'), may hold values from -6 to 6
- metric_x: float32 [1024, 128], P('elem', 'sub'), may hold values from 0.5 to 2
- metric_y: float32 [1024, 128], P('elem', 'sub'), may hold values from 0.5 to 2
- mass_weight: float32 [1024, 128], P('elem', 'sub'), may hold values from 0.5 to 2
- mass_inverse: float32 [1024, 128], P('elem', 'sub'), may hold values from 0.25 to 1
- phys_slot: int32 [32768], P(('elem', 'sub')), may hold values from 0 to 32767, as said below
- diff_inverse: bfloat16 [2048, 128, 128], P(('elem', 'sub')), may hold values from -0.1 to 0.8
- span_cost: int32 [2048], P(('elem', 'sub')), may hold values from 1 to 4, as said below
Outputs:
- tracers_out: bfloat16 [1024, 128, 1024], P('elem', 'sub')
The draws below stay inside these ranges and needn't reach their ends.
Inputs may be any that keep to these rules, and one draw needn't show every extreme that they name: `phys_slot`: A permutation of the columns. Every device sends exactly 4 of its columns to each of 64 devices (slot // 256 is the device of a slot) and none to the others, and every device receives exactly 256 columns. `span_cost`: 4 is reached in every draw.
All inputs are finite; a program needn't handle non-finite values.
Results may differ from the reference program's by a relative error of at most 0.009.
Values may be sent and summed in bfloat16 or wider, within the bound.
No kernel may reach another device: no remote copies, remote signals or barrier semaphores. Data moves between devices by JAX's collectives and lax.ppermute only.
A program may use at most 64 MiB of HBM per device.

```python
import math
import jax
import jax.numpy as jnp
import numpy as np
from jax import lax

LEV = 128
TRC = 8
KMAX = 4
PCOLS = 16
EX = 8
EY = 8
PX = 1024
PY = 128
NC = 256
COLS = 32768
SPANS = 2048
CAP = 4
N_ELEM = 32
N_SUB = 4


def draw_phys_slot(key, part):
    device_count = COLS // NC
    group_count = NC // CAP
    first_key, second_key, third_key = jax.random.split(jax.random.fold_in(key, 17), 3)
    scores = jax.random.permutation(first_key, device_count).astype(jnp.int32)
    device_ids = jnp.arange(device_count)
    scores = jnp.where(device_ids == 1, -3, jnp.where(device_ids == device_count - 1, -2, jnp.where(device_ids == device_count // 2, -1, scores)))
    offsets = jnp.argsort(scores)[:group_count]
    source_perm = jax.vmap(lambda sub_key: jax.random.permutation(sub_key, NC))(jax.random.split(second_key, device_count))
    target_perm = jax.vmap(lambda sub_key: jax.random.permutation(sub_key, NC))(jax.random.split(third_key, device_count))
    column = jnp.arange(COLS)
    source = column // NC
    position = source_perm.reshape(-1)
    group_index = position // CAP
    within = position % CAP
    target = (source + offsets[group_index]) % device_count
    arrival = group_index * CAP + within
    slot_index = target * NC + target_perm[target, arrival]
    return slot_index.astype(jnp.int32)


def draw_span_cost(key, part):
    per_device = NC // PCOLS
    device_count = SPANS // per_device
    key_one, key_two, key_three, key_four = jax.random.split(jax.random.fold_in(key, 23), 4)
    ceiling = jax.random.randint(key_one, (device_count,), 1, KMAX + 1)
    busiest = jax.random.randint(key_two, (), 0, device_count)
    ceiling = jnp.where(jnp.arange(device_count) == busiest, KMAX, ceiling)
    lowered = jax.random.randint(key_three, (SPANS,), 0, 2)
    forced = busiest * per_device + jax.random.randint(key_four, (), 0, per_device)
    lowered = jnp.where(jnp.arange(SPANS) == forced, 0, lowered)
    cost_value = jnp.maximum(ceiling[jnp.arange(SPANS) // per_device] - lowered, 1)
    return cost_value.astype(jnp.int32)


def draw_diff_inverse(key, part):
    key_one, key_two = jax.random.split(jax.random.fold_in(key, 31), 2)
    spread_scale = 0.2 / math.sqrt(LEV)
    off_diag = jnp.clip(jax.random.normal(key_one, (SPANS, LEV, LEV), jnp.float32) * spread_scale, -0.095, 0.095)
    diagonal_part = jax.random.uniform(key_two, (SPANS, LEV), jnp.float32, 0.55, 0.79)
    identity = jnp.eye(LEV, dtype=jnp.float32)
    return (off_diag * (1.0 - identity)[None] + identity[None] * diagonal_part[:, :, None]).astype(jnp.bfloat16)


def levels(own_key, dims, cuts, least, top_value):
    factor_of = 1.0
    for dim, shards_of in cuts:
        steps = jax.random.uniform(jax.random.fold_in(jax.random.fold_in(own_key, 6), dim), (shards_of,), jnp.float32, least / len(cuts), top_value / len(cuts))
        factor_of = factor_of * jnp.repeat(jnp.exp(steps), dims[dim] // shards_of).reshape((-1,) + (1,) * (len(dims) - 1 - dim))
    return factor_of


def scatter_about(own_key, extent, spread, reach, shards=(), kind=jnp.bfloat16):
    factor_of = levels(own_key, extent, shards, -0.22, 0.18) if shards else 1.0
    values = jax.random.normal(own_key, extent, jnp.float32) * spread * factor_of
    return jnp.minimum(jnp.maximum(values, -reach), reach).astype(kind)


def setup_inputs(seed: int = 0) -> dict:
    splits = jax.random.split(jax.random.key(seed), 9)
    return {
        "tracers": scatter_about(splits[0], (PX, PY, TRC * LEV), 1.0, 6.0, ((0, 32), (1, 4))),
        "metric_x": jnp.clip(jnp.exp(math.log(2.0) - 1.3862944 * jax.random.uniform(splits[1], (PX, PY), jnp.float32) ** levels(splits[1], (PX, PY), ((0, 32), (1, 4)), -0.2, 0.2)), 0.5, 2.0),
        "metric_y": jnp.clip(jnp.exp(math.log(2.0) - 1.3862944 * jax.random.uniform(splits[2], (PX, PY), jnp.float32) ** levels(splits[2], (PX, PY), ((0, 32), (1, 4)), -0.2, 0.2)), 0.5, 2.0),
        "mass_weight": jnp.clip(jnp.exp(math.log(2.0) - 1.3862944 * jax.random.uniform(splits[3], (PX, PY), jnp.float32) ** levels(splits[3], (PX, PY), ((0, 32), (1, 4)), -0.2, 0.2)), 0.5, 2.0),
        "mass_inverse": jnp.clip(jnp.exp(math.log(1.0) - 1.3862944 * jax.random.uniform(splits[4], (PX, PY), jnp.float32) ** levels(splits[4], (PX, PY), ((0, 32), (1, 4)), -0.2, 0.2)), 0.25, 1.0),
        "phys_slot": draw_phys_slot(jax.random.fold_in(splits[8], 71), 0),
        "diff_inverse": draw_diff_inverse(jax.random.fold_in(splits[8], 71), 0),
        "span_cost": draw_span_cost(jax.random.fold_in(splits[8], 71), 0),
    }


diffusion_nu = 0.01

def gll_matrix():
    gll_nodes = np.array([-1.0, -1.0 / math.sqrt(5.0), 1.0 / math.sqrt(5.0), 1.0])
    result = np.zeros((4, 4))
    for row_node in range(4):
        for col_node in range(4):
            if row_node == col_node:
                total = 0.0
                for other_node in range(4):
                    if other_node != row_node:
                        total += 1.0 / (gll_nodes[row_node] - gll_nodes[other_node])
                result[row_node, col_node] = total
            else:
                product_top = 1.0
                product_low = 1.0
                for other_node in range(4):
                    if other_node != col_node:
                        product_low *= gll_nodes[col_node] - gll_nodes[other_node]
                        if other_node != row_node:
                            product_top *= gll_nodes[row_node] - gll_nodes[other_node]
                result[row_node, col_node] = product_top / product_low
    return result

def contract(pattern, left_side, right_side):
    return jnp.einsum(pattern, left_side, right_side, precision=lax.Precision.HIGHEST)

def local_section(values, metric_x, metric_y):
    elem_rows = values.shape[0] // 4
    elem_cols = values.shape[1] // 4
    features = values.shape[2]
    derivative = jnp.asarray(gll_matrix(), dtype=jnp.float32)
    blocks = values.astype(jnp.float32).reshape(elem_rows, 4, elem_cols, 4, features)
    scale_x = metric_x.reshape(elem_rows, 4, elem_cols, 4, 1)
    scale_y = metric_y.reshape(elem_rows, 4, elem_cols, 4, 1)
    slope_x = contract('im,ambjf->aibjf', derivative, blocks)
    weak_x = contract('ki,akbjf->aibjf', derivative, scale_x * slope_x)
    slope_y = contract('jm,aibmf->aibjf', derivative, blocks)
    weak_y = contract('kj,aibkf->aibjf', derivative, scale_y * slope_y)
    section_field = blocks - diffusion_nu * (weak_x + weak_y)
    return section_field.reshape(values.shape)

def edge_masks(point_count):
    position = jnp.arange(point_count) % 4
    return ((position == 0).astype(jnp.float32), (position == 3).astype(jnp.float32))

def reference(tracers, metric_x, metric_y, mass_weight, mass_inverse, phys_slot, diff_inverse, span_cost):
    point_rows, point_cols, features = tracers.shape
    section_field = lax.map(lambda piece: local_section(piece[0], piece[1], piece[2]), (tracers.reshape(N_ELEM, -1, point_cols, features), metric_x.reshape(N_ELEM, -1, point_cols), metric_y.reshape(N_ELEM, -1, point_cols))).reshape(point_rows, point_cols, features)
    weighted = mass_weight[:, :, None] * section_field
    first_row, last_row = edge_masks(point_rows)
    along_x = weighted + first_row[:, None, None] * jnp.roll(weighted, 1, axis=0) + last_row[:, None, None] * jnp.roll(weighted, -1, axis=0)
    first_col, last_col = edge_masks(point_cols)
    summed = along_x + first_col[None, :, None] * jnp.roll(along_x, 1, axis=1) + last_col[None, :, None] * jnp.roll(along_x, -1, axis=1)
    settled = (mass_inverse[:, :, None] * summed).astype(jnp.bfloat16)
    settled_wide = settled.astype(jnp.float32)
    numerator = (mass_weight[:, :, None] * settled_wide).reshape(point_rows // 2, 2, point_cols // 2, 2, features).sum(axis=(1, 3))
    denominator = mass_weight.reshape(point_rows // 2, 2, point_cols // 2, 2).sum(axis=(1, 3))
    column_grid = (numerator / denominator[:, :, None]).astype(jnp.bfloat16)
    columns = column_grid.reshape(N_ELEM, 2 * EX, N_SUB, 2 * EY, features).transpose(0, 2, 1, 3, 4).reshape(COLS, features)
    slot_state = jnp.zeros((COLS, features), jnp.bfloat16).at[phys_slot].set(columns)
    start_state = slot_state.reshape(SPANS, PCOLS * TRC, LEV)
    inverse_wide = diff_inverse.astype(jnp.float32)
    current = start_state
    for step_index in range(KMAX):
        updated = contract('crm,clm->crl', current.astype(jnp.float32), inverse_wide).astype(jnp.bfloat16)
        current = jnp.where((step_index < span_cost)[:, None, None], updated, current)
    tendency = (current.astype(jnp.float32) - start_state.astype(jnp.float32)).astype(jnp.bfloat16).reshape(COLS, features)
    by_column = tendency[phys_slot]
    tend_grid = by_column.reshape(N_ELEM, N_SUB, 2 * EX, 2 * EY, features).transpose(0, 2, 1, 3, 4).reshape(point_rows // 2, point_cols // 2, features)
    spread_back = jnp.broadcast_to(tend_grid[:, None, :, None, :], (point_rows // 2, 2, point_cols // 2, 2, features)).reshape(point_rows, point_cols, features)
    return (settled_wide + spread_back.astype(jnp.float32)).astype(jnp.bfloat16)
```

```python
import math

import jax
import jax.numpy as jnp
import numpy as np
from jax import lax
from jax.experimental import pallas as pl
from jax.experimental.pallas import tpu as pltpu
from jax.sharding import PartitionSpec as P

diffusion_nu = 0.01
LANES = 128


def gll_matrix():
    gll_nodes = np.array([-1.0, -1.0 / math.sqrt(5.0), 1.0 / math.sqrt(5.0), 1.0])
    result = np.zeros((4, 4))
    for row_node in range(4):
        for col_node in range(4):
            if row_node == col_node:
                total = 0.0
                for other_node in range(4):
                    if other_node != row_node:
                        total += 1.0 / (gll_nodes[row_node] - gll_nodes[other_node])
                result[row_node, col_node] = total
            else:
                product_top = 1.0
                product_low = 1.0
                for other_node in range(4):
                    if other_node != col_node:
                        product_low *= gll_nodes[col_node] - gll_nodes[other_node]
                        if other_node != row_node:
                            product_top *= gll_nodes[row_node] - gll_nodes[other_node]
                result[row_node, col_node] = product_top / product_low
    return result


DERIV = [[float(np.float32(v)) for v in row] for row in gll_matrix()]


def mix(coefs, terms):
    total = coefs[0] * terms[0]
    for c, t in zip(coefs[1:], terms[1:]):
        total = total + c * t
    return total


def section_kernel(q_ref, coef_ref, w_ref, rt_ref, rb_ref, cl_ref, cr_ref, s_ref):
    s_ref[...] = q_ref[...].astype(jnp.float32)
    d = DERIV

    def body(a, carry):
        q = [[s_ref[4 * a + i, pl.ds(j, 8, stride=4), :] for j in range(4)] for i in range(4)]
        mx = [[coef_ref[0, i, j, a] for j in range(4)] for i in range(4)]
        my = [[coef_ref[1, i, j, a] for j in range(4)] for i in range(4)]
        mw = [[coef_ref[2, i, j, a] for j in range(4)] for i in range(4)]
        tx = [
            [mx[k][j] * mix(d[k], [q[m][j] for m in range(4)]) for j in range(4)]
            for k in range(4)
        ]
        ty = [
            [my[i][k] * mix(d[k], [q[i][m] for m in range(4)]) for k in range(4)]
            for i in range(4)
        ]
        for i in range(4):
            for j in range(4):
                wx = mix([d[k][i] for k in range(4)], [tx[k][j] for k in range(4)])
                wy = mix([d[k][j] for k in range(4)], [ty[i][k] for k in range(4)])
                w_ref[i, j, a] = mw[i][j] * (q[i][j] - diffusion_nu * (wx + wy))
        return carry

    lax.fori_loop(0, 8, body, 0)
    for j in range(4):
        rt_ref[j] = w_ref[0, j, 0]
        rb_ref[j] = w_ref[3, j, 7]
    for i in range(4):
        for a in range(8):
            cl_ref[i, pl.ds(a, 1), :] = w_ref[i, 0, a, pl.ds(0, 1), :]
            cr_ref[i, pl.ds(a, 1), :] = w_ref[i, 3, a, pl.ds(7, 1), :]


def settle_kernel(
    w_ref, top_ref, bot_ref, lax_ref, rax_ref, coef_ref, den_ref, st_ref, col_ref, ss_ref
):
    sub = lax.broadcasted_iota(jnp.int32, (8, LANES), 0)

    def body(a, carry):
        x = [[w_ref[i, j, a] for j in range(4)] for i in range(4)]
        up = [
            jnp.where(a == 0, top_ref[j], w_ref[3, j, jnp.maximum(a - 1, 0)]) for j in range(4)
        ]
        dn = [
            jnp.where(a == 7, bot_ref[j], w_ref[0, j, jnp.minimum(a + 1, 7)]) for j in range(4)
        ]
        ax = [
            [x[0][j] + up[j] for j in range(4)],
            x[1],
            x[2],
            [x[3][j] + dn[j] for j in range(4)],
        ]
        settled = [[None] * 4 for _ in range(4)]
        for i in range(4):
            left = lax_ref[i, pl.ds(a, 1), :]
            right = rax_ref[i, pl.ds(a, 1), :]
            prev3 = jnp.where(sub == 0, left, pltpu.roll(ax[i][3], 1, 0))
            next0 = jnp.where(sub == 7, right, pltpu.roll(ax[i][0], 7, 0))
            summed = [ax[i][0] + prev3, ax[i][1], ax[i][2], ax[i][3] + next0]
            for j in range(4):
                value = (coef_ref[1, i, j, a] * summed[j]).astype(jnp.bfloat16)
                settled[i][j] = value.astype(jnp.float32)
                ss_ref[4 * a + i, pl.ds(j, 8, stride=4), :] = settled[i][j]
        for p in range(2):
            for q in range(2):
                num = None
                for i in (2 * p, 2 * p + 1):
                    for j in (2 * q, 2 * q + 1):
                        term = coef_ref[0, i, j, a] * settled[i][j]
                        num = term if num is None else num + term
                col_ref[a, p, q] = num / den_ref[p, q, a]
        return carry

    lax.fori_loop(0, 8, body, 0)
    st_ref[...] = ss_ref[...].astype(st_ref.dtype)


def finish_kernel(st_ref, tend_ref, out_ref, t2_ref):
    def body(r2, carry):
        t = tend_ref[pl.ds(pl.multiple_of(r2 * 16, 16), 16), :]
        t2_ref[pl.ds(0, 16, stride=2), :] = t
        t2_ref[pl.ds(1, 16, stride=2), :] = t
        spread = t2_ref[...]
        for half in range(2):
            row = 2 * r2 + half
            out_ref[row] = (st_ref[row].astype(jnp.float32) + spread).astype(out_ref.dtype)
        return carry

    lax.fori_loop(0, 16, body, 0)


def spec(shape, lane_axis=None):
    nd = len(shape)

    def index(h):
        return tuple(h if d == lane_axis else 0 for d in range(nd))

    return pl.BlockSpec(shape, index)


def run_section(tracers, coef):
    rows, cols, features = tracers.shape
    nb = features // LANES
    return pl.pallas_call(
        section_kernel,
        grid=(nb,),
        in_specs=[
            spec((rows, cols, LANES), 2),
            pl.BlockSpec((3, 4, 4, 8, 8, LANES), lambda h: (0, 0, 0, 0, 0, 0)),
        ],
        out_specs=[
            spec((4, 4, 8, 8, LANES), 4),
            spec((4, 8, LANES), 2),
            spec((4, 8, LANES), 2),
            spec((4, 8, LANES), 2),
            spec((4, 8, LANES), 2),
        ],
        out_shape=[
            jax.ShapeDtypeStruct((4, 4, 8, 8, features), jnp.float32),
            jax.ShapeDtypeStruct((4, 8, features), jnp.float32),
            jax.ShapeDtypeStruct((4, 8, features), jnp.float32),
            jax.ShapeDtypeStruct((4, 8, features), jnp.float32),
            jax.ShapeDtypeStruct((4, 8, features), jnp.float32),
        ],
        scratch_shapes=[pltpu.VMEM((rows, cols, LANES), jnp.float32)],
    )(tracers, coef)


def run_settle(w, top, bot, lax_halo, rax_halo, coef, den):
    features = w.shape[-1]
    nb = features // LANES
    return pl.pallas_call(
        settle_kernel,
        grid=(nb,),
        in_specs=[
            spec((4, 4, 8, 8, LANES), 4),
            spec((4, 8, LANES), 2),
            spec((4, 8, LANES), 2),
            spec((4, 8, LANES), 2),
            spec((4, 8, LANES), 2),
            pl.BlockSpec((2, 4, 4, 8, 8, LANES), lambda h: (1, 0, 0, 0, 0, 0)),
            spec((2, 2, 8, 8, LANES)),
        ],
        out_specs=[
            spec((32, 32, LANES), 2),
            spec((8, 2, 2, 8, LANES), 4),
        ],
        out_shape=[
            jax.ShapeDtypeStruct((32, 32, features), jnp.bfloat16),
            jax.ShapeDtypeStruct((8, 2, 2, 8, features), jnp.float32),
        ],
        scratch_shapes=[pltpu.VMEM((32, 32, LANES), jnp.float32)],
    )(w, top, bot, lax_halo, rax_halo, coef, den)


def run_finish(settled, tend):
    rows, cols, features = settled.shape
    nb = features // LANES
    return pl.pallas_call(
        finish_kernel,
        grid=(nb,),
        in_specs=[spec((rows, cols, LANES), 2), spec((tend.shape[0], LANES), 1)],
        out_specs=spec((rows, cols, LANES), 2),
        out_shape=jax.ShapeDtypeStruct(settled.shape, jnp.bfloat16),
        scratch_shapes=[pltpu.VMEM((cols, LANES), jnp.float32)],
    )(settled, tend)


def deinterleave(field):
    return field.reshape(8, 4, 8, 4).transpose(1, 3, 0, 2)


def shift(x, axis, step):
    count = lax.axis_size(axis)
    return lax.ppermute(x, axis, [(k, (k + step) % count) for k in range(count)])


def shift2(x, step_e, step_s):
    ne = lax.axis_size("elem")
    ns = lax.axis_size("sub")
    pairs = []
    for e in range(ne):
        for s in range(ns):
            pairs.append((e * ns + s, ((e + step_e) % ne) * ns + (s + step_s) % ns))
    return lax.ppermute(x, ("elem", "sub"), pairs)


def on_device(
    tracers, metric_x, metric_y, mass_weight, mass_inverse, phys_slot, diff_inverse, span_cost
):
    point_rows, point_cols, features = tracers.shape
    coef = jnp.broadcast_to(
        jnp.stack(
            [deinterleave(metric_x), deinterleave(metric_y), deinterleave(mass_weight),
             deinterleave(mass_inverse)]
        )[..., None],
        (4, 4, 4, 8, 8, LANES),
    )
    den = mass_weight.reshape(8, 2, 2, 8, 2, 2).sum(axis=(2, 5)).transpose(1, 3, 0, 2)
    den = jnp.broadcast_to(den[..., None], (2, 2, 8, 8, LANES))

    w, rt, rb, cl, cr = run_section(tracers, coef)
    top = shift(rb, "elem", 1)
    bot = shift(rt, "elem", -1)
    left = shift(cr, "sub", 1)
    right = shift(cl, "sub", -1)
    corner_tl = shift2(rb[3, 7], 1, 1)
    corner_tr = shift2(rb[0, 0], 1, -1)
    corner_bl = shift2(rt[3, 7], -1, 1)
    corner_br = shift2(rt[0, 0], -1, -1)

    def along_x(side, above, below):
        first = side[0] + jnp.concatenate([above[None], side[3, :-1]], axis=0)
        last = side[3] + jnp.concatenate([side[0, 1:], below[None]], axis=0)
        return jnp.stack([first, side[1], side[2], last])

    lax_halo = along_x(left, corner_tl, corner_bl)
    rax_halo = along_x(right, corner_tr, corner_br)
    settled, columns = run_settle(w, top, bot, lax_halo, rax_halo, coef, den)
    columns = columns.reshape(-1, features).astype(jnp.bfloat16)

    column_count = columns.shape[0]
    slot_k = phys_slot.reshape(8, 2, 8, 2).transpose(0, 1, 3, 2).reshape(-1)
    device_count = lax.axis_size(("elem", "sub"))
    capacity = max(1, 2 * column_count // device_count)
    slot_total = device_count * capacity
    target = slot_k // column_count
    landing = slot_k % column_count
    column_order = jnp.arange(column_count)
    earlier = (target[None, :] == target[:, None]) & (column_order[None, :] < column_order[:, None])
    position = jnp.sum(earlier.astype(jnp.int32), axis=1)
    dest_row = target * capacity + position
    slot_order = jnp.arange(slot_total)
    send_table = (slot_order[:, None] == dest_row[None, :]).astype(jnp.bfloat16)
    outgoing = jnp.dot(send_table, columns, preferred_element_type=jnp.float32).astype(jnp.bfloat16)
    label_values = jnp.dot(
        send_table.astype(jnp.float32),
        (landing + 1).astype(jnp.float32),
        precision=lax.Precision.HIGHEST,
    )
    labels = label_values.astype(jnp.int32) - 1
    outgoing = outgoing.reshape(device_count, capacity, features)
    labels = labels.reshape(device_count, capacity)
    arrived, arrived_labels = (
        lax.all_to_all(outgoing, ("elem", "sub"), split_axis=0, concat_axis=0, tiled=True),
        lax.all_to_all(labels, ("elem", "sub"), split_axis=0, concat_axis=0, tiled=True),
    )
    arrived = arrived.reshape(-1, features)
    arrived_labels = arrived_labels.reshape(-1)
    place_table = (column_order[:, None] == arrived_labels[None, :]).astype(jnp.bfloat16)
    slot_state = jnp.dot(place_table, arrived, preferred_element_type=jnp.float32).astype(
        jnp.bfloat16
    )
    span_count = span_cost.shape[0]
    levels = diff_inverse.shape[1]
    start_state = slot_state.reshape(span_count, -1, levels)

    def substep(step_index, current):
        updated = jnp.einsum(
            "crm,clm->crl", current, diff_inverse, preferred_element_type=jnp.float32
        ).astype(jnp.bfloat16)
        return jnp.where((step_index < span_cost)[:, None, None], updated, current)

    final_state = lax.fori_loop(0, jnp.max(span_cost), substep, start_state)
    tendency = (
        (final_state.astype(jnp.float32) - start_state.astype(jnp.float32))
        .astype(jnp.bfloat16)
        .reshape(column_count, features)
    )
    reply_table = (arrived_labels[:, None] == column_order[None, :]).astype(jnp.bfloat16)
    replies = jnp.dot(reply_table, tendency, preferred_element_type=jnp.float32).astype(
        jnp.bfloat16
    )
    replies = replies.reshape(device_count, capacity, features)
    returned = lax.all_to_all(replies, ("elem", "sub"), split_axis=0, concat_axis=0, tiled=True)
    returned = returned.reshape(slot_total, features)
    dest_nat = dest_row.reshape(8, 2, 2, 8).transpose(0, 1, 3, 2).reshape(-1)
    back_table = (dest_nat[:, None] == slot_order[None, :]).astype(jnp.bfloat16)
    tend_cols = jnp.dot(back_table, returned, preferred_element_type=jnp.float32)
    return run_finish(settled, tend_cols)


def solution(mesh):
    in_specs = (
        P("elem", "sub", None),
        P("elem", "sub"),
        P("elem", "sub"),
        P("elem", "sub"),
        P("elem", "sub"),
        P(("elem", "sub")),
        P(("elem", "sub"), None, None),
        P(("elem", "sub")),
    )
    out_specs = P("elem", "sub", None)
    return jax.shard_map(
        on_device, mesh=mesh, in_specs=in_specs, out_specs=out_specs, check_vma=False
    )
```

```python
import math

import jax
import jax.numpy as jnp
import numpy as np
from jax import lax
from jax.experimental import pallas as pl
from jax.experimental.pallas import tpu as pltpu
from jax.sharding import PartitionSpec as P

diffusion_nu = 0.01
LANES = 128


def gll_matrix():
    gll_nodes = np.array([-1.0, -1.0 / math.sqrt(5.0), 1.0 / math.sqrt(5.0), 1.0])
    result = np.zeros((4, 4))
    for row_node in range(4):
        for col_node in range(4):
            if row_node == col_node:
                total = 0.0
                for other_node in range(4):
                    if other_node != row_node:
                        total += 1.0 / (gll_nodes[row_node] - gll_nodes[other_node])
                result[row_node, col_node] = total
            else:
                product_top = 1.0
                product_low = 1.0
                for other_node in range(4):
                    if other_node != col_node:
                        product_low *= gll_nodes[col_node] - gll_nodes[other_node]
                        if other_node != row_node:
                            product_top *= gll_nodes[row_node] - gll_nodes[other_node]
                result[row_node, col_node] = product_top / product_low
    return result


DERIV = [[float(np.float32(v)) for v in row] for row in gll_matrix()]


def mix(coefs, terms):
    total = coefs[0] * terms[0]
    for c, t in zip(coefs[1:], terms[1:]):
        total = total + c * t
    return total


def section_kernel(q_ref, coef_ref, w_ref, rt_ref, rb_ref, cl_ref, cr_ref, s_ref):
    s_ref[...] = q_ref[...].astype(jnp.float32)
    d = DERIV

    def body(a, carry):
        q = [[s_ref[4 * a + i, pl.ds(j, 8, stride=4), :] for j in range(4)] for i in range(4)]
        mx = [[coef_ref[0, i, j, a] for j in range(4)] for i in range(4)]
        my = [[coef_ref[1, i, j, a] for j in range(4)] for i in range(4)]
        mw = [[coef_ref[2, i, j, a] for j in range(4)] for i in range(4)]
        tx = [
            [mx[k][j] * mix(d[k], [q[m][j] for m in range(4)]) for j in range(4)]
            for k in range(4)
        ]
        ty = [
            [my[i][k] * mix(d[k], [q[i][m] for m in range(4)]) for k in range(4)]
            for i in range(4)
        ]
        for i in range(4):
            for j in range(4):
                wx = mix([d[k][i] for k in range(4)], [tx[k][j] for k in range(4)])
                wy = mix([d[k][j] for k in range(4)], [ty[i][k] for k in range(4)])
                w_ref[i, j, a] = mw[i][j] * (q[i][j] - diffusion_nu * (wx + wy))
        return carry

    lax.fori_loop(0, 8, body, 0)
    for j in range(4):
        rt_ref[j] = w_ref[0, j, 0]
        rb_ref[j] = w_ref[3, j, 7]
    for i in range(4):
        for a in range(8):
            cl_ref[i, pl.ds(a, 1), :] = w_ref[i, 0, a, pl.ds(0, 1), :]
            cr_ref[i, pl.ds(a, 1), :] = w_ref[i, 3, a, pl.ds(7, 1), :]


def settle_kernel(
    w_ref, top_ref, bot_ref, lax_ref, rax_ref, coef_ref, den_ref, st_ref, col_ref, ss_ref
):
    sub = lax.broadcasted_iota(jnp.int32, (8, LANES), 0)

    def body(a, carry):
        x = [[w_ref[i, j, a] for j in range(4)] for i in range(4)]
        up = [
            jnp.where(a == 0, top_ref[j], w_ref[3, j, jnp.maximum(a - 1, 0)]) for j in range(4)
        ]
        dn = [
            jnp.where(a == 7, bot_ref[j], w_ref[0, j, jnp.minimum(a + 1, 7)]) for j in range(4)
        ]
        ax = [
            [x[0][j] + up[j] for j in range(4)],
            x[1],
            x[2],
            [x[3][j] + dn[j] for j in range(4)],
        ]
        settled = [[None] * 4 for _ in range(4)]
        for i in range(4):
            left = lax_ref[i, pl.ds(a, 1), :]
            right = rax_ref[i, pl.ds(a, 1), :]
            prev3 = jnp.where(sub == 0, left, pltpu.roll(ax[i][3], 1, 0))
            next0 = jnp.where(sub == 7, right, pltpu.roll(ax[i][0], 7, 0))
            summed = [ax[i][0] + prev3, ax[i][1], ax[i][2], ax[i][3] + next0]
            for j in range(4):
                value = (coef_ref[1, i, j, a] * summed[j]).astype(jnp.bfloat16)
                settled[i][j] = value.astype(jnp.float32)
                ss_ref[4 * a + i, pl.ds(j, 8, stride=4), :] = settled[i][j]
        for p in range(2):
            for q in range(2):
                num = None
                for i in (2 * p, 2 * p + 1):
                    for j in (2 * q, 2 * q + 1):
                        term = coef_ref[0, i, j, a] * settled[i][j]
                        num = term if num is None else num + term
                col_ref[a, p, q] = num / den_ref[p, q, a]
        return carry

    lax.fori_loop(0, 8, body, 0)
    st_ref[...] = ss_ref[...].astype(st_ref.dtype)


def finish_kernel(st_ref, tend_ref, out_ref, t2_ref):
    chunks = tend_ref.shape[1] // LANES

    def body(r2, carry):
        for h in range(chunks):
            lanes = pl.ds(h * LANES, LANES)
            t = tend_ref[pl.ds(pl.multiple_of(r2 * 16, 16), 16), lanes]
            t2_ref[h, pl.ds(0, 16, stride=2), :] = t
            t2_ref[h, pl.ds(1, 16, stride=2), :] = t
            spread = t2_ref[h]
            for half in range(2):
                row = 2 * r2 + half
                out_ref[row, :, lanes] = (
                    st_ref[row, :, lanes].astype(jnp.float32) + spread
                ).astype(out_ref.dtype)
        return carry

    lax.fori_loop(0, 16, body, 0)


def spec(shape, lane_axis=None):
    nd = len(shape)

    def index(h):
        return tuple(h if d == lane_axis else 0 for d in range(nd))

    return pl.BlockSpec(shape, index)


def run_section(tracers, coef):
    rows, cols, features = tracers.shape
    nb = features // LANES
    return pl.pallas_call(
        section_kernel,
        grid=(nb,),
        in_specs=[
            spec((rows, cols, LANES), 2),
            pl.BlockSpec((3, 4, 4, 8, 8, LANES), lambda h: (0, 0, 0, 0, 0, 0)),
        ],
        out_specs=[
            spec((4, 4, 8, 8, LANES), 4),
            spec((4, 8, LANES), 2),
            spec((4, 8, LANES), 2),
            spec((4, 8, LANES), 2),
            spec((4, 8, LANES), 2),
        ],
        out_shape=[
            jax.ShapeDtypeStruct((4, 4, 8, 8, features), jnp.float32),
            jax.ShapeDtypeStruct((4, 8, features), jnp.float32),
            jax.ShapeDtypeStruct((4, 8, features), jnp.float32),
            jax.ShapeDtypeStruct((4, 8, features), jnp.float32),
            jax.ShapeDtypeStruct((4, 8, features), jnp.float32),
        ],
        scratch_shapes=[pltpu.VMEM((rows, cols, LANES), jnp.float32)],
    )(tracers, coef)


def run_settle(w, top, bot, lax_halo, rax_halo, coef, den):
    features = w.shape[-1]
    nb = features // LANES
    return pl.pallas_call(
        settle_kernel,
        grid=(nb,),
        in_specs=[
            spec((4, 4, 8, 8, LANES), 4),
            spec((4, 8, LANES), 2),
            spec((4, 8, LANES), 2),
            spec((4, 8, LANES), 2),
            spec((4, 8, LANES), 2),
            pl.BlockSpec((2, 4, 4, 8, 8, LANES), lambda h: (1, 0, 0, 0, 0, 0)),
            spec((2, 2, 8, 8, LANES)),
        ],
        out_specs=[
            spec((32, 32, LANES), 2),
            spec((8, 2, 2, 8, LANES), 4),
        ],
        out_shape=[
            jax.ShapeDtypeStruct((32, 32, features), jnp.bfloat16),
            jax.ShapeDtypeStruct((8, 2, 2, 8, features), jnp.float32),
        ],
        scratch_shapes=[pltpu.VMEM((32, 32, LANES), jnp.float32)],
    )(w, top, bot, lax_halo, rax_halo, coef, den)


def run_finish(settled, tend):
    rows, cols, features = settled.shape
    width = 4 * LANES
    nb = features // width
    return pl.pallas_call(
        finish_kernel,
        grid=(nb,),
        in_specs=[spec((rows, cols, width), 2), spec((tend.shape[0], width), 1)],
        out_specs=spec((rows, cols, width), 2),
        out_shape=jax.ShapeDtypeStruct(settled.shape, jnp.bfloat16),
        scratch_shapes=[pltpu.VMEM((width // LANES, cols, LANES), jnp.float32)],
    )(settled, tend)


def deinterleave(field):
    return field.reshape(8, 4, 8, 4).transpose(1, 3, 0, 2)


def shift(x, axis, step):
    count = lax.axis_size(axis)
    return lax.ppermute(x, axis, [(k, (k + step) % count) for k in range(count)])


def on_device(
    tracers, metric_x, metric_y, mass_weight, mass_inverse, phys_slot, diff_inverse, span_cost
):
    point_rows, point_cols, features = tracers.shape
    coef = jnp.broadcast_to(
        jnp.stack(
            [deinterleave(metric_x), deinterleave(metric_y), deinterleave(mass_weight),
             deinterleave(mass_inverse)]
        )[..., None],
        (4, 4, 4, 8, 8, LANES),
    )
    den = mass_weight.reshape(8, 2, 2, 8, 2, 2).sum(axis=(2, 5)).transpose(1, 3, 0, 2)
    den = jnp.broadcast_to(den[..., None], (2, 2, 8, 8, LANES))

    w, rt, rb, cl, cr = run_section(tracers, coef)
    top = shift(rb, "elem", 1)
    bot = shift(rt, "elem", -1)

    def along_x(side, above, below):
        first = side[0] + jnp.concatenate([above[None], side[3, :-1]], axis=0)
        last = side[3] + jnp.concatenate([side[0, 1:], below[None]], axis=0)
        return jnp.stack([first, side[1], side[2], last])

    lax_halo = shift(along_x(cr, top[3, 7], bot[3, 7]), "sub", 1)
    rax_halo = shift(along_x(cl, top[0, 0], bot[0, 0]), "sub", -1)
    settled, columns = run_settle(w, top, bot, lax_halo, rax_halo, coef, den)
    columns = columns.reshape(-1, features).astype(jnp.bfloat16)

    column_count = columns.shape[0]
    slot_k = phys_slot.reshape(8, 2, 8, 2).transpose(0, 1, 3, 2).reshape(-1)
    device_count = lax.axis_size(("elem", "sub"))
    capacity = max(1, 2 * column_count // device_count)
    slot_total = device_count * capacity
    target = slot_k // column_count
    landing = slot_k % column_count
    column_order = jnp.arange(column_count)
    earlier = (target[None, :] == target[:, None]) & (column_order[None, :] < column_order[:, None])
    position = jnp.sum(earlier.astype(jnp.int32), axis=1)
    dest_row = target * capacity + position
    slot_order = jnp.arange(slot_total)
    send_table = (slot_order[:, None] == dest_row[None, :]).astype(jnp.bfloat16)
    label_block = jnp.where(
        jnp.arange(LANES)[None, :] == 0, (landing + 1)[:, None].astype(jnp.bfloat16), 0
    ).astype(jnp.bfloat16)
    payload = jnp.concatenate([columns, label_block], axis=1)
    outgoing = jnp.dot(send_table, payload, preferred_element_type=jnp.float32).astype(jnp.bfloat16)
    outgoing = outgoing.reshape(device_count, capacity, features + LANES)
    arrived = lax.all_to_all(outgoing, ("elem", "sub"), split_axis=0, concat_axis=0, tiled=True)
    arrived = arrived.reshape(-1, features + LANES)
    arrived_labels = arrived[:, features].astype(jnp.int32) - 1
    arrived = arrived[:, :features]
    place_table = (column_order[:, None] == arrived_labels[None, :]).astype(jnp.bfloat16)
    slot_state = jnp.dot(place_table, arrived, preferred_element_type=jnp.float32).astype(
        jnp.bfloat16
    )
    span_count = span_cost.shape[0]
    levels = diff_inverse.shape[1]
    start_state = slot_state.reshape(span_count, -1, levels)

    def substep(step_index, current):
        updated = jnp.einsum(
            "crm,clm->crl", current, diff_inverse, preferred_element_type=jnp.float32
        ).astype(jnp.bfloat16)
        return jnp.where((step_index < span_cost)[:, None, None], updated, current)

    final_state = lax.fori_loop(0, jnp.max(span_cost), substep, start_state)
    tendency = (
        (final_state.astype(jnp.float32) - start_state.astype(jnp.float32))
        .astype(jnp.bfloat16)
        .reshape(column_count, features)
    )
    reply_table = (arrived_labels[:, None] == column_order[None, :]).astype(jnp.bfloat16)
    replies = jnp.dot(reply_table, tendency, preferred_element_type=jnp.float32).astype(
        jnp.bfloat16
    )
    replies = replies.reshape(device_count, capacity, features)
    returned = lax.all_to_all(replies, ("elem", "sub"), split_axis=0, concat_axis=0, tiled=True)
    returned = returned.reshape(slot_total, features)
    dest_nat = dest_row.reshape(8, 2, 2, 8).transpose(0, 1, 3, 2).reshape(-1)
    back_table = (dest_nat[:, None] == slot_order[None, :]).astype(jnp.bfloat16)
    tend_cols = jnp.dot(back_table, returned, preferred_element_type=jnp.float32)
    return run_finish(settled, tend_cols)


def solution(mesh):
    in_specs = (
        P("elem", "sub", None),
        P("elem", "sub"),
        P("elem", "sub"),
        P("elem", "sub"),
        P("elem", "sub"),
        P(("elem", "sub")),
        P(("elem", "sub"), None, None),
        P(("elem", "sub")),
    )
    out_specs = P("elem", "sub", None)
    return jax.shard_map(
        on_device, mesh=mesh, in_specs=in_specs, out_specs=out_specs, check_vma=False
    )
```

```python
import math

import jax
import jax.numpy as jnp
import numpy as np
from jax import lax
from jax.experimental import pallas as pl
from jax.experimental.pallas import tpu as pltpu
from jax.sharding import PartitionSpec as P

diffusion_nu = 0.01
LANES = 128


def gll_matrix():
    gll_nodes = np.array([-1.0, -1.0 / math.sqrt(5.0), 1.0 / math.sqrt(5.0), 1.0])
    result = np.zeros((4, 4))
    for row_node in range(4):
        for col_node in range(4):
            if row_node == col_node:
                total = 0.0
                for other_node in range(4):
                    if other_node != row_node:
                        total += 1.0 / (gll_nodes[row_node] - gll_nodes[other_node])
                result[row_node, col_node] = total
            else:
                product_top = 1.0
                product_low = 1.0
                for other_node in range(4):
                    if other_node != col_node:
                        product_low *= gll_nodes[col_node] - gll_nodes[other_node]
                        if other_node != row_node:
                            product_top *= gll_nodes[row_node] - gll_nodes[other_node]
                result[row_node, col_node] = product_top / product_low
    return result


DERIV = [[float(np.float32(v)) for v in row] for row in gll_matrix()]


def mix(coefs, terms):
    total = coefs[0] * terms[0]
    for c, t in zip(coefs[1:], terms[1:]):
        total = total + c * t
    return total


def section_kernel(q_ref, coef_ref, w_ref, rt_ref, rb_ref, cl_ref, cr_ref, s_ref):
    s_ref[...] = q_ref[...].astype(jnp.float32)
    d = DERIV

    def body(a, carry):
        q = [[s_ref[4 * a + i, pl.ds(j, 8, stride=4), :] for j in range(4)] for i in range(4)]
        mx, my, mw = (
            [[coef_ref[kind, 4 * a + i, pl.ds(j, 8, stride=4), :] for j in range(4)]
             for i in range(4)]
            for kind in range(3)
        )
        tx = [
            [mx[k][j] * mix(d[k], [q[m][j] for m in range(4)]) for j in range(4)]
            for k in range(4)
        ]
        ty = [
            [my[i][k] * mix(d[k], [q[i][m] for m in range(4)]) for k in range(4)]
            for i in range(4)
        ]
        for i in range(4):
            for j in range(4):
                wx = mix([d[k][i] for k in range(4)], [tx[k][j] for k in range(4)])
                wy = mix([d[k][j] for k in range(4)], [ty[i][k] for k in range(4)])
                w_ref[i, j, a] = mw[i][j] * (q[i][j] - diffusion_nu * (wx + wy))
        return carry

    lax.fori_loop(0, 8, body, 0)
    for j in range(4):
        rt_ref[j] = w_ref[0, j, 0]
        rb_ref[j] = w_ref[3, j, 7]
    for i in range(4):
        for a in range(8):
            cl_ref[i, pl.ds(a, 1), :] = w_ref[i, 0, a, pl.ds(0, 1), :]
            cr_ref[i, pl.ds(a, 1), :] = w_ref[i, 3, a, pl.ds(7, 1), :]


def settle_kernel(w_ref, top_ref, bot_ref, lax_ref, rax_ref, coef_ref, st_ref, col_ref, ss_ref):
    sub = lax.broadcasted_iota(jnp.int32, (8, LANES), 0)

    def body(a, carry):
        x = [[w_ref[i, j, a] for j in range(4)] for i in range(4)]
        mw = [[coef_ref[0, 4 * a + i, pl.ds(j, 8, stride=4), :] for j in range(4)] for i in range(4)]
        mi = [[coef_ref[1, 4 * a + i, pl.ds(j, 8, stride=4), :] for j in range(4)] for i in range(4)]
        up = [
            jnp.where(a == 0, top_ref[j], w_ref[3, j, jnp.maximum(a - 1, 0)]) for j in range(4)
        ]
        dn = [
            jnp.where(a == 7, bot_ref[j], w_ref[0, j, jnp.minimum(a + 1, 7)]) for j in range(4)
        ]
        ax = [
            [x[0][j] + up[j] for j in range(4)],
            x[1],
            x[2],
            [x[3][j] + dn[j] for j in range(4)],
        ]
        settled = [[None] * 4 for _ in range(4)]
        for i in range(4):
            left = lax_ref[i, pl.ds(a, 1), :]
            right = rax_ref[i, pl.ds(a, 1), :]
            prev3 = jnp.where(sub == 0, left, pltpu.roll(ax[i][3], 1, 0))
            next0 = jnp.where(sub == 7, right, pltpu.roll(ax[i][0], 7, 0))
            summed = [ax[i][0] + prev3, ax[i][1], ax[i][2], ax[i][3] + next0]
            for j in range(4):
                value = (mi[i][j] * summed[j]).astype(jnp.bfloat16)
                settled[i][j] = value.astype(jnp.float32)
                ss_ref[4 * a + i, pl.ds(j, 8, stride=4), :] = settled[i][j]
        for p in range(2):
            pair = []
            for q in range(2):
                num = None
                den = None
                for i in (2 * p, 2 * p + 1):
                    for j in (2 * q, 2 * q + 1):
                        term = mw[i][j] * settled[i][j]
                        num = term if num is None else num + term
                        den = mw[i][j] if den is None else den + mw[i][j]
                pair.append(num / den)
            row = pl.multiple_of((a * 2 + p) * 16, 16)
            col_ref[pl.ds(row, 16), :] = jnp.concatenate(pair, axis=0).astype(col_ref.dtype)
        return carry

    lax.fori_loop(0, 8, body, 0)
    st_ref[...] = ss_ref[...].astype(st_ref.dtype)


def finish_kernel(st_ref, tend_ref, out_ref, t2_ref):
    chunks = tend_ref.shape[1] // LANES

    def body(r2, carry):
        for h in range(chunks):
            lanes = pl.ds(h * LANES, LANES)
            t = tend_ref[pl.ds(pl.multiple_of(r2 * 16, 16), 16), lanes]
            t2_ref[h, pl.ds(0, 16, stride=2), :] = t
            t2_ref[h, pl.ds(1, 16, stride=2), :] = t
            spread = t2_ref[h]
            for half in range(2):
                row = 2 * r2 + half
                out_ref[row, :, lanes] = (
                    st_ref[row, :, lanes].astype(jnp.float32) + spread
                ).astype(out_ref.dtype)
        return carry

    lax.fori_loop(0, 16, body, 0)


def spec(shape, lane_axis=None):
    nd = len(shape)

    def index(h):
        return tuple(h if d == lane_axis else 0 for d in range(nd))

    return pl.BlockSpec(shape, index)


def run_section(tracers, coef):
    rows, cols, features = tracers.shape
    nb = features // LANES
    return pl.pallas_call(
        section_kernel,
        grid=(nb,),
        in_specs=[
            spec((rows, cols, LANES), 2),
            pl.BlockSpec((3, rows, cols, LANES), lambda h: (0, 0, 0, 0)),
        ],
        out_specs=[
            spec((4, 4, 8, 8, LANES), 4),
            spec((4, 8, LANES), 2),
            spec((4, 8, LANES), 2),
            spec((4, 8, LANES), 2),
            spec((4, 8, LANES), 2),
        ],
        out_shape=[
            jax.ShapeDtypeStruct((4, 4, 8, 8, features), jnp.float32),
            jax.ShapeDtypeStruct((4, 8, features), jnp.float32),
            jax.ShapeDtypeStruct((4, 8, features), jnp.float32),
            jax.ShapeDtypeStruct((4, 8, features), jnp.float32),
            jax.ShapeDtypeStruct((4, 8, features), jnp.float32),
        ],
        scratch_shapes=[pltpu.VMEM((rows, cols, LANES), jnp.float32)],
    )(tracers, coef)


def run_settle(w, top, bot, lax_halo, rax_halo, coef):
    features = w.shape[-1]
    nb = features // LANES
    return pl.pallas_call(
        settle_kernel,
        grid=(nb,),
        in_specs=[
            spec((4, 4, 8, 8, LANES), 4),
            spec((4, 8, LANES), 2),
            spec((4, 8, LANES), 2),
            spec((4, 8, LANES), 2),
            spec((4, 8, LANES), 2),
            pl.BlockSpec((2, 32, 32, LANES), lambda h: (1, 0, 0, 0)),
        ],
        out_specs=[
            spec((32, 32, LANES), 2),
            spec((256, LANES), 1),
        ],
        out_shape=[
            jax.ShapeDtypeStruct((32, 32, features), jnp.bfloat16),
            jax.ShapeDtypeStruct((256, features), jnp.bfloat16),
        ],
        scratch_shapes=[pltpu.VMEM((32, 32, LANES), jnp.float32)],
    )(w, top, bot, lax_halo, rax_halo, coef)


def run_finish(settled, tend):
    rows, cols, features = settled.shape
    width = 4 * LANES
    nb = features // width
    return pl.pallas_call(
        finish_kernel,
        grid=(nb,),
        in_specs=[spec((rows, cols, width), 2), spec((tend.shape[0], width), 1)],
        out_specs=spec((rows, cols, width), 2),
        out_shape=jax.ShapeDtypeStruct(settled.shape, jnp.bfloat16),
        scratch_shapes=[pltpu.VMEM((width // LANES, cols, LANES), jnp.float32)],
    )(settled, tend)


def shift(x, axis, step):
    count = lax.axis_size(axis)
    return lax.ppermute(x, axis, [(k, (k + step) % count) for k in range(count)])


def on_device(
    tracers, metric_x, metric_y, mass_weight, mass_inverse, phys_slot, diff_inverse, span_cost
):
    point_rows, point_cols, features = tracers.shape
    coef = jnp.broadcast_to(
        jnp.stack([metric_x, metric_y, mass_weight, mass_inverse])[..., None],
        (4, point_rows, point_cols, LANES),
    )

    w, rt, rb, cl, cr = run_section(tracers, coef)
    top = shift(rb, "elem", 1)
    bot = shift(rt, "elem", -1)

    def along_x(side, above, below):
        first = side[0] + jnp.concatenate([above[None], side[3, :-1]], axis=0)
        last = side[3] + jnp.concatenate([side[0, 1:], below[None]], axis=0)
        return jnp.stack([first, side[1], side[2], last])

    lax_halo = shift(along_x(cr, top[3, 7], bot[3, 7]), "sub", 1)
    rax_halo = shift(along_x(cl, top[0, 0], bot[0, 0]), "sub", -1)
    settled, columns = run_settle(w, top, bot, lax_halo, rax_halo, coef)

    column_count = columns.shape[0]
    slot_k = phys_slot.reshape(8, 2, 8, 2).transpose(0, 1, 3, 2).reshape(-1)
    device_count = lax.axis_size(("elem", "sub"))
    capacity = max(1, 2 * column_count // device_count)
    slot_total = device_count * capacity
    target = slot_k // column_count
    landing = slot_k % column_count
    column_order = jnp.arange(column_count)
    earlier = (target[None, :] == target[:, None]) & (column_order[None, :] < column_order[:, None])
    position = jnp.sum(earlier.astype(jnp.int32), axis=1)
    dest_row = target * capacity + position
    slot_order = jnp.arange(slot_total)
    send_table = (slot_order[:, None] == dest_row[None, :]).astype(jnp.bfloat16)
    label_block = jnp.where(
        jnp.arange(LANES)[None, :] == 0, (landing + 1)[:, None].astype(jnp.bfloat16), 0
    ).astype(jnp.bfloat16)
    payload = jnp.concatenate([columns, label_block], axis=1)
    outgoing = jnp.dot(send_table, payload, preferred_element_type=jnp.float32).astype(jnp.bfloat16)
    outgoing = outgoing.reshape(device_count, capacity, features + LANES)
    arrived = lax.all_to_all(outgoing, ("elem", "sub"), split_axis=0, concat_axis=0, tiled=True)
    arrived = arrived.reshape(-1, features + LANES)
    arrived_labels = arrived[:, features].astype(jnp.int32) - 1
    arrived = arrived[:, :features]
    place_table = (column_order[:, None] == arrived_labels[None, :]).astype(jnp.bfloat16)
    slot_state = jnp.dot(place_table, arrived, preferred_element_type=jnp.float32).astype(
        jnp.bfloat16
    )
    span_count = span_cost.shape[0]
    levels = diff_inverse.shape[1]
    start_state = slot_state.reshape(span_count, -1, levels)

    def substep(step_index, current):
        updated = jnp.einsum(
            "crm,clm->crl", current, diff_inverse, preferred_element_type=jnp.float32
        ).astype(jnp.bfloat16)
        return jnp.where((step_index < span_cost)[:, None, None], updated, current)

    final_state = lax.fori_loop(0, jnp.max(span_cost), substep, start_state)
    tendency = (
        (final_state.astype(jnp.float32) - start_state.astype(jnp.float32))
        .astype(jnp.bfloat16)
        .reshape(column_count, features)
    )
    reply_table = (arrived_labels[:, None] == column_order[None, :]).astype(jnp.bfloat16)
    replies = jnp.dot(reply_table, tendency, preferred_element_type=jnp.float32).astype(
        jnp.bfloat16
    )
    replies = replies.reshape(device_count, capacity, features)
    returned = lax.all_to_all(replies, ("elem", "sub"), split_axis=0, concat_axis=0, tiled=True)
    returned = returned.reshape(slot_total, features)
    dest_nat = dest_row.reshape(8, 2, 2, 8).transpose(0, 1, 3, 2).reshape(-1)
    back_table = (dest_nat[:, None] == slot_order[None, :]).astype(jnp.bfloat16)
    tend_cols = jnp.dot(back_table, returned, preferred_element_type=jnp.float32)
    return run_finish(settled, tend_cols)


def solution(mesh):
    in_specs = (
        P("elem", "sub", None),
        P("elem", "sub"),
        P("elem", "sub"),
        P("elem", "sub"),
        P("elem", "sub"),
        P(("elem", "sub")),
        P(("elem", "sub"), None, None),
        P(("elem", "sub")),
    )
    out_specs = P("elem", "sub", None)
    return jax.shard_map(
        on_device, mesh=mesh, in_specs=in_specs, out_specs=out_specs, check_vma=False
    )
```

```python
import math

import jax
import jax.numpy as jnp
import numpy as np
from jax import lax
from jax.experimental import pallas as pl
from jax.experimental.pallas import tpu as pltpu
from jax.sharding import PartitionSpec as P

diffusion_nu = 0.01
LANES = 128


def gll_matrix():
    gll_nodes = np.array([-1.0, -1.0 / math.sqrt(5.0), 1.0 / math.sqrt(5.0), 1.0])
    result = np.zeros((4, 4))
    for row_node in range(4):
        for col_node in range(4):
            if row_node == col_node:
                total = 0.0
                for other_node in range(4):
                    if other_node != row_node:
                        total += 1.0 / (gll_nodes[row_node] - gll_nodes[other_node])
                result[row_node, col_node] = total
            else:
                product_top = 1.0
                product_low = 1.0
                for other_node in range(4):
                    if other_node != col_node:
                        product_low *= gll_nodes[col_node] - gll_nodes[other_node]
                        if other_node != row_node:
                            product_top *= gll_nodes[row_node] - gll_nodes[other_node]
                result[row_node, col_node] = product_top / product_low
    return result


DERIV = [[float(np.float32(v)) for v in row] for row in gll_matrix()]


def mix(coefs, terms):
    total = coefs[0] * terms[0]
    for c, t in zip(coefs[1:], terms[1:]):
        total = total + c * t
    return total


def section_kernel(q_ref, coef_ref, w_ref, rt_ref, rb_ref, cl_ref, cr_ref, s_ref):
    s_ref[...] = q_ref[...].astype(jnp.float32)
    d = DERIV

    def body(a, carry):
        q = [[s_ref[4 * a + i, pl.ds(j, 8, stride=4), :] for j in range(4)] for i in range(4)]
        mx, my, mw = (
            [[coef_ref[kind, 4 * a + i, pl.ds(j, 8, stride=4), :] for j in range(4)]
             for i in range(4)]
            for kind in range(3)
        )
        tx = [
            [mx[k][j] * mix(d[k], [q[m][j] for m in range(4)]) for j in range(4)]
            for k in range(4)
        ]
        ty = [
            [my[i][k] * mix(d[k], [q[i][m] for m in range(4)]) for k in range(4)]
            for i in range(4)
        ]
        for i in range(4):
            for j in range(4):
                wx = mix([d[k][i] for k in range(4)], [tx[k][j] for k in range(4)])
                wy = mix([d[k][j] for k in range(4)], [ty[i][k] for k in range(4)])
                w_ref[i, j, a] = mw[i][j] * (q[i][j] - diffusion_nu * (wx + wy))
        return carry

    lax.fori_loop(0, 8, body, 0)
    for j in range(4):
        rt_ref[j] = w_ref[0, j, 0]
        rb_ref[j] = w_ref[3, j, 7]
    for i in range(4):
        for a in range(8):
            cl_ref[i, pl.ds(a, 1), :] = w_ref[i, 0, a, pl.ds(0, 1), :]
            cr_ref[i, pl.ds(a, 1), :] = w_ref[i, 3, a, pl.ds(7, 1), :]


def settle_kernel(w_ref, top_ref, bot_ref, lax_ref, rax_ref, coef_ref, st_ref, col_ref, ss_ref):
    sub = lax.broadcasted_iota(jnp.int32, (8, LANES), 0)

    def body(a, carry):
        x = [[w_ref[i, j, a] for j in range(4)] for i in range(4)]
        mw = [[coef_ref[0, 4 * a + i, pl.ds(j, 8, stride=4), :] for j in range(4)] for i in range(4)]
        mi = [[coef_ref[1, 4 * a + i, pl.ds(j, 8, stride=4), :] for j in range(4)] for i in range(4)]
        up = [
            jnp.where(a == 0, top_ref[j], w_ref[3, j, jnp.maximum(a - 1, 0)]) for j in range(4)
        ]
        dn = [
            jnp.where(a == 7, bot_ref[j], w_ref[0, j, jnp.minimum(a + 1, 7)]) for j in range(4)
        ]
        ax = [
            [x[0][j] + up[j] for j in range(4)],
            x[1],
            x[2],
            [x[3][j] + dn[j] for j in range(4)],
        ]
        settled = [[None] * 4 for _ in range(4)]
        for i in range(4):
            left = lax_ref[i, pl.ds(a, 1), :]
            right = rax_ref[i, pl.ds(a, 1), :]
            prev3 = jnp.where(sub == 0, left, pltpu.roll(ax[i][3], 1, 0))
            next0 = jnp.where(sub == 7, right, pltpu.roll(ax[i][0], 7, 0))
            summed = [ax[i][0] + prev3, ax[i][1], ax[i][2], ax[i][3] + next0]
            for j in range(4):
                value = (mi[i][j] * summed[j]).astype(jnp.bfloat16)
                settled[i][j] = value.astype(jnp.float32)
                ss_ref[4 * a + i, pl.ds(j, 8, stride=4), :] = settled[i][j]
        for p in range(2):
            pair = []
            for q in range(2):
                num = None
                den = None
                for i in (2 * p, 2 * p + 1):
                    for j in (2 * q, 2 * q + 1):
                        term = mw[i][j] * settled[i][j]
                        num = term if num is None else num + term
                        den = mw[i][j] if den is None else den + mw[i][j]
                pair.append(num / den)
            row = pl.multiple_of((a * 2 + p) * 16, 16)
            col_ref[pl.ds(row, 16), :] = jnp.concatenate(pair, axis=0).astype(col_ref.dtype)
        return carry

    lax.fori_loop(0, 8, body, 0)
    st_ref[...] = ss_ref[...].astype(st_ref.dtype)


def finish_kernel(st_ref, tend_ref, out_ref, t2_ref):
    chunks = tend_ref.shape[1] // LANES

    def body(r2, carry):
        for h in range(chunks):
            lanes = pl.ds(h * LANES, LANES)
            t = tend_ref[pl.ds(pl.multiple_of(r2 * 16, 16), 16), lanes]
            t2_ref[h, pl.ds(0, 16, stride=2), :] = t
            t2_ref[h, pl.ds(1, 16, stride=2), :] = t
            spread = t2_ref[h]
            for half in range(2):
                row = 2 * r2 + half
                out_ref[row, :, lanes] = (
                    st_ref[row, :, lanes].astype(jnp.float32) + spread
                ).astype(out_ref.dtype)
        return carry

    lax.fori_loop(0, 16, body, 0)


def edge_kernel(cl_ref, cr_ref, top_ref, bot_ref, lsend_ref, rsend_ref):
    sub = lax.broadcasted_iota(jnp.int32, cl_ref.shape[1:], 0)
    for side_ref, out_ref, b, j in ((cr_ref, lsend_ref, 7, 3), (cl_ref, rsend_ref, 0, 0)):
        above = top_ref[j, pl.ds(b, 1), :]
        below = bot_ref[j, pl.ds(b, 1), :]
        first = side_ref[0] + jnp.where(sub == 0, above, pltpu.roll(side_ref[3], 1, 0))
        last = side_ref[3] + jnp.where(sub == 7, below, pltpu.roll(side_ref[0], 7, 0))
        out_ref[0] = first
        out_ref[1] = side_ref[1]
        out_ref[2] = side_ref[2]
        out_ref[3] = last


def run_edges(cl, cr, top, bot):
    return pl.pallas_call(
        edge_kernel,
        out_shape=[jax.ShapeDtypeStruct(cl.shape, cl.dtype)] * 2,
    )(cl, cr, top, bot)


def diffusion_kernel(cost_ref, place_ref, arrived_ref, inv_ref, reply_ref, out_ref, slot_ref, tend_ref):
    slot_ref[...] = jnp.dot(
        place_ref[...], arrived_ref[:, pl.ds(0, slot_ref.shape[1])],
        preferred_element_type=jnp.float32,
    ).astype(slot_ref.dtype)
    span_slots = slot_ref.shape[0] // inv_ref.shape[0]
    steps = 4

    def body(span, carry):
        rows = pl.ds(pl.multiple_of(span * span_slots, span_slots), span_slots)
        tracers = slot_ref.shape[1] // LANES
        start = jnp.concatenate(
            [slot_ref[rows, pl.ds(t * LANES, LANES)] for t in range(tracers)], axis=0
        )
        inverse = inv_ref[span]
        cost = cost_ref[span]
        current = start
        for step in range(steps):
            updated = lax.dot_general(
                current, inverse, (((1,), (1,)), ((), ())), preferred_element_type=jnp.float32
            ).astype(current.dtype)
            current = jnp.where(step < cost, updated, current)
        tend = (current.astype(jnp.float32) - start.astype(jnp.float32)).astype(tend_ref.dtype)
        for t in range(tracers):
            tend_ref[rows, pl.ds(t * LANES, LANES)] = tend[t * span_slots:(t + 1) * span_slots]
        return carry

    lax.fori_loop(0, inv_ref.shape[0], body, 0)
    out_ref[...] = jnp.dot(
        reply_ref[...], tend_ref[...], preferred_element_type=jnp.float32
    ).astype(out_ref.dtype)


def run_diffusion(span_cost, place, arrived, inverse, reply, features):
    slots = place.shape[0]
    vmem = pltpu.VMEM
    return pl.pallas_call(
        diffusion_kernel,
        in_specs=[pl.BlockSpec(memory_space=pltpu.SMEM)] + [pl.BlockSpec(memory_space=vmem)] * 4,
        out_specs=pl.BlockSpec(memory_space=vmem),
        out_shape=jax.ShapeDtypeStruct((reply.shape[0], features), jnp.bfloat16),
        scratch_shapes=[vmem((slots, features), jnp.bfloat16), vmem((slots, features), jnp.bfloat16)],
    )(span_cost, place, arrived, inverse, reply)


def spec(shape, lane_axis=None):
    nd = len(shape)

    def index(h):
        return tuple(h if d == lane_axis else 0 for d in range(nd))

    return pl.BlockSpec(shape, index)


def run_section(tracers, coef):
    rows, cols, features = tracers.shape
    nb = features // LANES
    return pl.pallas_call(
        section_kernel,
        grid=(nb,),
        in_specs=[
            spec((rows, cols, LANES), 2),
            pl.BlockSpec((3, rows, cols, LANES), lambda h: (0, 0, 0, 0)),
        ],
        out_specs=[
            spec((4, 4, 8, 8, LANES), 4),
            spec((4, 8, LANES), 2),
            spec((4, 8, LANES), 2),
            spec((4, 8, LANES), 2),
            spec((4, 8, LANES), 2),
        ],
        out_shape=[
            jax.ShapeDtypeStruct((4, 4, 8, 8, features), jnp.float32),
            jax.ShapeDtypeStruct((4, 8, features), jnp.float32),
            jax.ShapeDtypeStruct((4, 8, features), jnp.float32),
            jax.ShapeDtypeStruct((4, 8, features), jnp.float32),
            jax.ShapeDtypeStruct((4, 8, features), jnp.float32),
        ],
        scratch_shapes=[pltpu.VMEM((rows, cols, LANES), jnp.float32)],
    )(tracers, coef)


def run_settle(w, top, bot, lax_halo, rax_halo, coef):
    features = w.shape[-1]
    nb = features // LANES
    return pl.pallas_call(
        settle_kernel,
        grid=(nb,),
        in_specs=[
            spec((4, 4, 8, 8, LANES), 4),
            spec((4, 8, LANES), 2),
            spec((4, 8, LANES), 2),
            spec((4, 8, LANES), 2),
            spec((4, 8, LANES), 2),
            pl.BlockSpec((2, 32, 32, LANES), lambda h: (1, 0, 0, 0)),
        ],
        out_specs=[
            spec((32, 32, LANES), 2),
            spec((256, LANES), 1),
        ],
        out_shape=[
            jax.ShapeDtypeStruct((32, 32, features), jnp.bfloat16),
            jax.ShapeDtypeStruct((256, features), jnp.bfloat16),
        ],
        scratch_shapes=[pltpu.VMEM((32, 32, LANES), jnp.float32)],
    )(w, top, bot, lax_halo, rax_halo, coef)


def run_finish(settled, tend):
    rows, cols, features = settled.shape
    width = 4 * LANES
    nb = features // width
    return pl.pallas_call(
        finish_kernel,
        grid=(nb,),
        in_specs=[spec((rows, cols, width), 2), spec((tend.shape[0], width), 1)],
        out_specs=spec((rows, cols, width), 2),
        out_shape=jax.ShapeDtypeStruct(settled.shape, jnp.bfloat16),
        scratch_shapes=[pltpu.VMEM((width // LANES, cols, LANES), jnp.float32)],
    )(settled, tend)


def shift(x, axis, step):
    count = lax.axis_size(axis)
    return lax.ppermute(x, axis, [(k, (k + step) % count) for k in range(count)])


def on_device(
    tracers, metric_x, metric_y, mass_weight, mass_inverse, phys_slot, diff_inverse, span_cost
):
    point_rows, point_cols, features = tracers.shape
    coef = jnp.broadcast_to(
        jnp.stack([metric_x, metric_y, mass_weight, mass_inverse])[..., None],
        (4, point_rows, point_cols, LANES),
    )

    w, rt, rb, cl, cr = run_section(tracers, coef)
    top = shift(rb, "elem", 1)
    bot = shift(rt, "elem", -1)

    lsend, rsend = run_edges(cl, cr, top, bot)
    lax_halo = shift(lsend, "sub", 1)
    rax_halo = shift(rsend, "sub", -1)
    settled, columns = run_settle(w, top, bot, lax_halo, rax_halo, coef)

    column_count = columns.shape[0]
    slot_k = phys_slot.reshape(8, 2, 8, 2).transpose(0, 1, 3, 2).reshape(-1)
    device_count = lax.axis_size(("elem", "sub"))
    capacity = max(1, 2 * column_count // device_count)
    slot_total = device_count * capacity
    target = slot_k // column_count
    landing = slot_k % column_count
    column_order = jnp.arange(column_count)
    earlier = (target[None, :] == target[:, None]) & (column_order[None, :] < column_order[:, None])
    position = jnp.sum(earlier.astype(jnp.int32), axis=1)
    dest_row = target * capacity + position
    slot_order = jnp.arange(slot_total)
    send_table = (slot_order[:, None] == dest_row[None, :]).astype(jnp.bfloat16)
    label_block = jnp.where(
        jnp.arange(LANES)[None, :] == 0, (landing + 1)[:, None].astype(jnp.bfloat16), 0
    ).astype(jnp.bfloat16)
    payload = jnp.concatenate([columns, label_block], axis=1)
    outgoing = jnp.einsum(
        "dck,kf->dcf", send_table.reshape(device_count, capacity, column_count), payload,
        preferred_element_type=jnp.float32,
    ).astype(jnp.bfloat16)
    arrived = lax.all_to_all(outgoing, ("elem", "sub"), split_axis=0, concat_axis=0, tiled=True)
    arrived = arrived.reshape(-1, features + LANES)
    arrived_labels = arrived[:, features].astype(jnp.int32) - 1
    place_table = (column_order[:, None] == arrived_labels[None, :]).astype(jnp.bfloat16)
    reply_table = (arrived_labels[:, None] == column_order[None, :]).astype(jnp.bfloat16)
    replies = run_diffusion(span_cost, place_table, arrived, diff_inverse, reply_table, features)
    replies = replies.reshape(device_count, capacity, features)
    returned = lax.all_to_all(replies, ("elem", "sub"), split_axis=0, concat_axis=0, tiled=True)
    returned = returned.reshape(slot_total, features)
    dest_nat = dest_row.reshape(8, 2, 2, 8).transpose(0, 1, 3, 2).reshape(-1)
    back_table = (dest_nat[:, None] == slot_order[None, :]).astype(jnp.bfloat16)
    tend_cols = jnp.dot(back_table, returned, preferred_element_type=jnp.float32)
    return run_finish(settled, tend_cols)


def solution(mesh):
    in_specs = (
        P("elem", "sub", None),
        P("elem", "sub"),
        P("elem", "sub"),
        P("elem", "sub"),
        P("elem", "sub"),
        P(("elem", "sub")),
        P(("elem", "sub"), None, None),
        P(("elem", "sub")),
    )
    out_specs = P("elem", "sub", None)
    return jax.shard_map(
        on_device, mesh=mesh, in_specs=in_specs, out_specs=out_specs, check_vma=False
    )
```

```python
import math

import jax
import jax.numpy as jnp
import numpy as np
from jax import lax
from jax.experimental import pallas as pl
from jax.experimental.pallas import tpu as pltpu
from jax.sharding import PartitionSpec as P

diffusion_nu = 0.01
LANES = 128


def gll_matrix():
    gll_nodes = np.array([-1.0, -1.0 / math.sqrt(5.0), 1.0 / math.sqrt(5.0), 1.0])
    result = np.zeros((4, 4))
    for row_node in range(4):
        for col_node in range(4):
            if row_node == col_node:
                total = 0.0
                for other_node in range(4):
                    if other_node != row_node:
                        total += 1.0 / (gll_nodes[row_node] - gll_nodes[other_node])
                result[row_node, col_node] = total
            else:
                product_top = 1.0
                product_low = 1.0
                for other_node in range(4):
                    if other_node != col_node:
                        product_low *= gll_nodes[col_node] - gll_nodes[other_node]
                        if other_node != row_node:
                            product_top *= gll_nodes[row_node] - gll_nodes[other_node]
                result[row_node, col_node] = product_top / product_low
    return result


DERIV = [[float(np.float32(v)) for v in row] for row in gll_matrix()]


def mix(coefs, terms):
    total = coefs[0] * terms[0]
    for c, t in zip(coefs[1:], terms[1:]):
        total = total + c * t
    return total


def section_kernel(q_ref, coef_ref, w_ref, rt_ref, rb_ref, cl_ref, cr_ref, s_ref):
    s_ref[...] = q_ref[...].astype(jnp.float32)
    d = DERIV

    def body(a, carry):
        q = [[s_ref[4 * a + i, pl.ds(j, 8, stride=4), :] for j in range(4)] for i in range(4)]
        mx, my, mw = (
            [[coef_ref[kind, 4 * a + i, pl.ds(j, 8, stride=4), :] for j in range(4)]
             for i in range(4)]
            for kind in range(3)
        )
        tx = [
            [mx[k][j] * mix(d[k], [q[m][j] for m in range(4)]) for j in range(4)]
            for k in range(4)
        ]
        ty = [
            [my[i][k] * mix(d[k], [q[i][m] for m in range(4)]) for k in range(4)]
            for i in range(4)
        ]
        for i in range(4):
            for j in range(4):
                wx = mix([d[k][i] for k in range(4)], [tx[k][j] for k in range(4)])
                wy = mix([d[k][j] for k in range(4)], [ty[i][k] for k in range(4)])
                w_ref[i, j, a] = mw[i][j] * (q[i][j] - diffusion_nu * (wx + wy))
        return carry

    lax.fori_loop(0, 8, body, 0)
    for j in range(4):
        rt_ref[j] = w_ref[0, j, 0]
        rb_ref[j] = w_ref[3, j, 7]
    for i in range(4):
        for a in range(8):
            cl_ref[i, pl.ds(a, 1), :] = w_ref[i, 0, a, pl.ds(0, 1), :]
            cr_ref[i, pl.ds(a, 1), :] = w_ref[i, 3, a, pl.ds(7, 1), :]


def settle_kernel(w_ref, top_ref, bot_ref, lax_ref, rax_ref, coef_ref, st_ref, col_ref, ss_ref):
    sub = lax.broadcasted_iota(jnp.int32, (8, LANES), 0)

    def body(a, carry):
        x = [[w_ref[i, j, a] for j in range(4)] for i in range(4)]
        mw = [[coef_ref[0, 4 * a + i, pl.ds(j, 8, stride=4), :] for j in range(4)] for i in range(4)]
        mi = [[coef_ref[1, 4 * a + i, pl.ds(j, 8, stride=4), :] for j in range(4)] for i in range(4)]
        up = [
            jnp.where(a == 0, top_ref[j], w_ref[3, j, jnp.maximum(a - 1, 0)]) for j in range(4)
        ]
        dn = [
            jnp.where(a == 7, bot_ref[j], w_ref[0, j, jnp.minimum(a + 1, 7)]) for j in range(4)
        ]
        ax = [
            [x[0][j] + up[j] for j in range(4)],
            x[1],
            x[2],
            [x[3][j] + dn[j] for j in range(4)],
        ]
        settled = [[None] * 4 for _ in range(4)]
        for i in range(4):
            left = lax_ref[i, pl.ds(a, 1), :]
            right = rax_ref[i, pl.ds(a, 1), :]
            prev3 = jnp.where(sub == 0, left, pltpu.roll(ax[i][3], 1, 0))
            next0 = jnp.where(sub == 7, right, pltpu.roll(ax[i][0], 7, 0))
            summed = [ax[i][0] + prev3, ax[i][1], ax[i][2], ax[i][3] + next0]
            for j in range(4):
                value = (mi[i][j] * summed[j]).astype(jnp.bfloat16)
                settled[i][j] = value.astype(jnp.float32)
                ss_ref[4 * a + i, pl.ds(j, 8, stride=4), :] = settled[i][j]
        for p in range(2):
            pair = []
            for q in range(2):
                num = None
                den = None
                for i in (2 * p, 2 * p + 1):
                    for j in (2 * q, 2 * q + 1):
                        term = mw[i][j] * settled[i][j]
                        num = term if num is None else num + term
                        den = mw[i][j] if den is None else den + mw[i][j]
                pair.append(num / den)
            row = pl.multiple_of((a * 2 + p) * 16, 16)
            col_ref[pl.ds(row, 16), :] = jnp.concatenate(pair, axis=0).astype(col_ref.dtype)
        return carry

    lax.fori_loop(0, 8, body, 0)
    st_ref[...] = ss_ref[...].astype(st_ref.dtype)


def finish_kernel(st_ref, tend_ref, out_ref, t2_ref):
    chunks = tend_ref.shape[1] // LANES

    def body(r2, carry):
        for h in range(chunks):
            lanes = pl.ds(h * LANES, LANES)
            t = tend_ref[pl.ds(pl.multiple_of(r2 * 16, 16), 16), lanes]
            t2_ref[h, pl.ds(0, 16, stride=2), :] = t
            t2_ref[h, pl.ds(1, 16, stride=2), :] = t
            spread = t2_ref[h]
            for half in range(2):
                row = 2 * r2 + half
                out_ref[row, :, lanes] = (
                    st_ref[row, :, lanes].astype(jnp.float32) + spread
                ).astype(out_ref.dtype)
        return carry

    lax.fori_loop(0, 16, body, 0)


def edge_kernel(cl_ref, cr_ref, top_ref, bot_ref, lsend_ref, rsend_ref):
    sub = lax.broadcasted_iota(jnp.int32, cl_ref.shape[1:], 0)
    for side_ref, out_ref, b, j in ((cr_ref, lsend_ref, 7, 3), (cl_ref, rsend_ref, 0, 0)):
        above = top_ref[j, pl.ds(b, 1), :]
        below = bot_ref[j, pl.ds(b, 1), :]
        first = side_ref[0] + jnp.where(sub == 0, above, pltpu.roll(side_ref[3], 1, 0))
        last = side_ref[3] + jnp.where(sub == 7, below, pltpu.roll(side_ref[0], 7, 0))
        out_ref[0] = first
        out_ref[1] = side_ref[1]
        out_ref[2] = side_ref[2]
        out_ref[3] = last


def run_edges(cl, cr, top, bot):
    return pl.pallas_call(
        edge_kernel,
        out_shape=[jax.ShapeDtypeStruct(cl.shape, cl.dtype)] * 2,
    )(cl, cr, top, bot)


def diffusion_kernel(cost_ref, place_ref, arrived_ref, inv_ref, reply_ref, out_ref, slot_ref, tend_ref):
    slot_ref[...] = jnp.dot(
        place_ref[...], arrived_ref[:, pl.ds(0, slot_ref.shape[1])],
        preferred_element_type=jnp.float32,
    ).astype(slot_ref.dtype)
    span_slots = slot_ref.shape[0] // inv_ref.shape[0]
    steps = 4

    tracers = slot_ref.shape[1] // LANES
    group = 4

    def body(g, carry):
        rows, starts, inverses, costs = [], [], [], []
        for u in range(group):
            span = g * group + u
            rows.append(pl.ds(pl.multiple_of(span * span_slots, span_slots), span_slots))
            starts.append(jnp.concatenate(
                [slot_ref[rows[u], pl.ds(t * LANES, LANES)] for t in range(tracers)], axis=0
            ))
            inverses.append(inv_ref[span])
            costs.append(cost_ref[span])
        current = list(starts)
        for step in range(steps):
            for u in range(group):
                updated = lax.dot_general(
                    current[u], inverses[u], (((1,), (1,)), ((), ())),
                    preferred_element_type=jnp.float32,
                ).astype(current[u].dtype)
                current[u] = jnp.where(step < costs[u], updated, current[u])
        for u in range(group):
            tend = (current[u].astype(jnp.float32) - starts[u].astype(jnp.float32)).astype(
                tend_ref.dtype
            )
            for t in range(tracers):
                tend_ref[rows[u], pl.ds(t * LANES, LANES)] = tend[t * span_slots:(t + 1) * span_slots]
        return carry

    lax.fori_loop(0, inv_ref.shape[0] // group, body, 0)
    out_ref[...] = jnp.dot(
        reply_ref[...], tend_ref[...], preferred_element_type=jnp.float32
    ).astype(out_ref.dtype)


def run_diffusion(span_cost, place, arrived, inverse, reply, features):
    slots = place.shape[0]
    vmem = pltpu.VMEM
    return pl.pallas_call(
        diffusion_kernel,
        in_specs=[pl.BlockSpec(memory_space=pltpu.SMEM)] + [pl.BlockSpec(memory_space=vmem)] * 4,
        out_specs=pl.BlockSpec(memory_space=vmem),
        out_shape=jax.ShapeDtypeStruct((reply.shape[0], features), jnp.bfloat16),
        scratch_shapes=[vmem((slots, features), jnp.bfloat16), vmem((slots, features), jnp.bfloat16)],
    )(span_cost, place, arrived, inverse, reply)


def spec(shape, lane_axis=None):
    nd = len(shape)

    def index(h):
        return tuple(h if d == lane_axis else 0 for d in range(nd))

    return pl.BlockSpec(shape, index)


def run_section(tracers, coef):
    rows, cols, features = tracers.shape
    nb = features // LANES
    return pl.pallas_call(
        section_kernel,
        grid=(nb,),
        in_specs=[
            spec((rows, cols, LANES), 2),
            pl.BlockSpec((3, rows, cols, LANES), lambda h: (0, 0, 0, 0)),
        ],
        out_specs=[
            spec((4, 4, 8, 8, LANES), 4),
            spec((4, 8, LANES), 2),
            spec((4, 8, LANES), 2),
            spec((4, 8, LANES), 2),
            spec((4, 8, LANES), 2),
        ],
        out_shape=[
            jax.ShapeDtypeStruct((4, 4, 8, 8, features), jnp.float32),
            jax.ShapeDtypeStruct((4, 8, features), jnp.float32),
            jax.ShapeDtypeStruct((4, 8, features), jnp.float32),
            jax.ShapeDtypeStruct((4, 8, features), jnp.float32),
            jax.ShapeDtypeStruct((4, 8, features), jnp.float32),
        ],
        scratch_shapes=[pltpu.VMEM((rows, cols, LANES), jnp.float32)],
    )(tracers, coef)


def run_settle(w, top, bot, lax_halo, rax_halo, coef):
    features = w.shape[-1]
    nb = features // LANES
    return pl.pallas_call(
        settle_kernel,
        grid=(nb,),
        in_specs=[
            spec((4, 4, 8, 8, LANES), 4),
            spec((4, 8, LANES), 2),
            spec((4, 8, LANES), 2),
            spec((4, 8, LANES), 2),
            spec((4, 8, LANES), 2),
            pl.BlockSpec((2, 32, 32, LANES), lambda h: (1, 0, 0, 0)),
        ],
        out_specs=[
            spec((32, 32, LANES), 2),
            spec((256, LANES), 1),
        ],
        out_shape=[
            jax.ShapeDtypeStruct((32, 32, features), jnp.bfloat16),
            jax.ShapeDtypeStruct((256, features), jnp.bfloat16),
        ],
        scratch_shapes=[pltpu.VMEM((32, 32, LANES), jnp.float32)],
    )(w, top, bot, lax_halo, rax_halo, coef)


def run_finish(settled, tend):
    rows, cols, features = settled.shape
    width = 4 * LANES
    nb = features // width
    return pl.pallas_call(
        finish_kernel,
        grid=(nb,),
        in_specs=[spec((rows, cols, width), 2), spec((tend.shape[0], width), 1)],
        out_specs=spec((rows, cols, width), 2),
        out_shape=jax.ShapeDtypeStruct(settled.shape, jnp.bfloat16),
        scratch_shapes=[pltpu.VMEM((width // LANES, cols, LANES), jnp.float32)],
    )(settled, tend)


def shift(x, axis, step):
    count = lax.axis_size(axis)
    return lax.ppermute(x, axis, [(k, (k + step) % count) for k in range(count)])


def on_device(
    tracers, metric_x, metric_y, mass_weight, mass_inverse, phys_slot, diff_inverse, span_cost
):
    point_rows, point_cols, features = tracers.shape
    coef = jnp.broadcast_to(
        jnp.stack([metric_x, metric_y, mass_weight, mass_inverse])[..., None],
        (4, point_rows, point_cols, LANES),
    )

    w, rt, rb, cl, cr = run_section(tracers, coef)
    top = shift(rb, "elem", 1)
    bot = shift(rt, "elem", -1)

    lsend, rsend = run_edges(cl, cr, top, bot)
    lax_halo = shift(lsend, "sub", 1)
    rax_halo = shift(rsend, "sub", -1)
    settled, columns = run_settle(w, top, bot, lax_halo, rax_halo, coef)

    column_count = columns.shape[0]
    slot_k = phys_slot.reshape(8, 2, 8, 2).transpose(0, 1, 3, 2).reshape(-1)
    device_count = lax.axis_size(("elem", "sub"))
    capacity = max(1, 2 * column_count // device_count)
    slot_total = device_count * capacity
    target = slot_k // column_count
    landing = slot_k % column_count
    column_order = jnp.arange(column_count)
    earlier = (target[None, :] == target[:, None]) & (column_order[None, :] < column_order[:, None])
    position = jnp.sum(earlier.astype(jnp.int32), axis=1)
    dest_row = target * capacity + position
    slot_order = jnp.arange(slot_total)
    send_table = (slot_order[:, None] == dest_row[None, :]).astype(jnp.bfloat16)
    label_block = jnp.where(
        jnp.arange(LANES)[None, :] == 0, (landing + 1)[:, None].astype(jnp.bfloat16), 0
    ).astype(jnp.bfloat16)
    payload = jnp.concatenate([columns, label_block], axis=1)
    outgoing = jnp.einsum(
        "dck,kf->dcf", send_table.reshape(device_count, capacity, column_count), payload,
        preferred_element_type=jnp.float32,
    ).astype(jnp.bfloat16)
    arrived = lax.all_to_all(outgoing, ("elem", "sub"), split_axis=0, concat_axis=0, tiled=True)
    arrived = arrived.reshape(-1, features + LANES)
    arrived_labels = arrived[:, features].astype(jnp.int32) - 1
    place_table = (column_order[:, None] == arrived_labels[None, :]).astype(jnp.bfloat16)
    reply_table = (arrived_labels[:, None] == column_order[None, :]).astype(jnp.bfloat16)
    replies = run_diffusion(span_cost, place_table, arrived, diff_inverse, reply_table, features)
    replies = replies.reshape(device_count, capacity, features)
    returned = lax.all_to_all(replies, ("elem", "sub"), split_axis=0, concat_axis=0, tiled=True)
    returned = returned.reshape(slot_total, features)
    dest_nat = dest_row.reshape(8, 2, 2, 8).transpose(0, 1, 3, 2).reshape(-1)
    back_table = (dest_nat[:, None] == slot_order[None, :]).astype(jnp.bfloat16)
    tend_cols = jnp.dot(back_table, returned, preferred_element_type=jnp.float32)
    return run_finish(settled, tend_cols)


def solution(mesh):
    in_specs = (
        P("elem", "sub", None),
        P("elem", "sub"),
        P("elem", "sub"),
        P("elem", "sub"),
        P("elem", "sub"),
        P(("elem", "sub")),
        P(("elem", "sub"), None, None),
        P(("elem", "sub")),
    )
    out_specs = P("elem", "sub", None)
    return jax.shard_map(
        on_device, mesh=mesh, in_specs=in_specs, out_specs=out_specs, check_vma=False
    )
```

```python
import math

import jax
import jax.numpy as jnp
import numpy as np
from jax import lax
from jax.experimental import pallas as pl
from jax.experimental.pallas import tpu as pltpu
from jax.sharding import PartitionSpec as P

diffusion_nu = 0.01
LANES = 128


def gll_matrix():
    gll_nodes = np.array([-1.0, -1.0 / math.sqrt(5.0), 1.0 / math.sqrt(5.0), 1.0])
    result = np.zeros((4, 4))
    for row_node in range(4):
        for col_node in range(4):
            if row_node == col_node:
                total = 0.0
                for other_node in range(4):
                    if other_node != row_node:
                        total += 1.0 / (gll_nodes[row_node] - gll_nodes[other_node])
                result[row_node, col_node] = total
            else:
                product_top = 1.0
                product_low = 1.0
                for other_node in range(4):
                    if other_node != col_node:
                        product_low *= gll_nodes[col_node] - gll_nodes[other_node]
                        if other_node != row_node:
                            product_top *= gll_nodes[row_node] - gll_nodes[other_node]
                result[row_node, col_node] = product_top / product_low
    return result


DERIV = [[float(np.float32(v)) for v in row] for row in gll_matrix()]


def mix(coefs, terms):
    total = coefs[0] * terms[0]
    for c, t in zip(coefs[1:], terms[1:]):
        total = total + c * t
    return total


def section_kernel(q_ref, coef_ref, w_ref, rt_ref, rb_ref, cl_ref, cr_ref, s_ref):
    s_ref[...] = q_ref[...].astype(jnp.float32)
    d = DERIV

    def body(a, carry):
        q = [[s_ref[4 * a + i, pl.ds(j, 8, stride=4), :] for j in range(4)] for i in range(4)]
        mx, my, mw = (
            [[coef_ref[kind, 4 * a + i, pl.ds(j, 8, stride=4), :] for j in range(4)]
             for i in range(4)]
            for kind in range(3)
        )
        tx = [
            [mx[k][j] * mix(d[k], [q[m][j] for m in range(4)]) for j in range(4)]
            for k in range(4)
        ]
        ty = [
            [my[i][k] * mix(d[k], [q[i][m] for m in range(4)]) for k in range(4)]
            for i in range(4)
        ]
        for i in range(4):
            for j in range(4):
                wx = mix([d[k][i] for k in range(4)], [tx[k][j] for k in range(4)])
                wy = mix([d[k][j] for k in range(4)], [ty[i][k] for k in range(4)])
                w_ref[i, j, a] = mw[i][j] * (q[i][j] - diffusion_nu * (wx + wy))
        return carry

    lax.fori_loop(0, 8, body, 0)
    for j in range(4):
        rt_ref[j] = w_ref[0, j, 0]
        rb_ref[j] = w_ref[3, j, 7]
    for i in range(4):
        for a in range(8):
            cl_ref[i, pl.ds(a, 1), :] = w_ref[i, 0, a, pl.ds(0, 1), :]
            cr_ref[i, pl.ds(a, 1), :] = w_ref[i, 3, a, pl.ds(7, 1), :]


def settle_kernel(w_ref, top_ref, bot_ref, lax_ref, rax_ref, coef_ref, st_ref, col_ref, ss_ref):
    sub = lax.broadcasted_iota(jnp.int32, (8, LANES), 0)

    def body(a, carry):
        x = [[w_ref[i, j, a] for j in range(4)] for i in range(4)]
        mw = [[coef_ref[0, 4 * a + i, pl.ds(j, 8, stride=4), :] for j in range(4)] for i in range(4)]
        mi = [[coef_ref[1, 4 * a + i, pl.ds(j, 8, stride=4), :] for j in range(4)] for i in range(4)]
        up = [
            jnp.where(a == 0, top_ref[j], w_ref[3, j, jnp.maximum(a - 1, 0)]) for j in range(4)
        ]
        dn = [
            jnp.where(a == 7, bot_ref[j], w_ref[0, j, jnp.minimum(a + 1, 7)]) for j in range(4)
        ]
        ax = [
            [x[0][j] + up[j] for j in range(4)],
            x[1],
            x[2],
            [x[3][j] + dn[j] for j in range(4)],
        ]
        settled = [[None] * 4 for _ in range(4)]
        for i in range(4):
            left = lax_ref[i, pl.ds(a, 1), :]
            right = rax_ref[i, pl.ds(a, 1), :]
            prev3 = jnp.where(sub == 0, left, pltpu.roll(ax[i][3], 1, 0))
            next0 = jnp.where(sub == 7, right, pltpu.roll(ax[i][0], 7, 0))
            summed = [ax[i][0] + prev3, ax[i][1], ax[i][2], ax[i][3] + next0]
            for j in range(4):
                value = (mi[i][j] * summed[j]).astype(jnp.bfloat16)
                settled[i][j] = value.astype(jnp.float32)
                ss_ref[4 * a + i, pl.ds(j, 8, stride=4), :] = settled[i][j]
        for p in range(2):
            pair = []
            for q in range(2):
                num = None
                den = None
                for i in (2 * p, 2 * p + 1):
                    for j in (2 * q, 2 * q + 1):
                        term = mw[i][j] * settled[i][j]
                        num = term if num is None else num + term
                        den = mw[i][j] if den is None else den + mw[i][j]
                pair.append(num / den)
            row = pl.multiple_of((a * 2 + p) * 16, 16)
            col_ref[pl.ds(row, 16), :] = jnp.concatenate(pair, axis=0).astype(col_ref.dtype)
        return carry

    lax.fori_loop(0, 8, body, 0)
    st_ref[...] = ss_ref[...].astype(st_ref.dtype)


def finish_kernel(st_ref, back_ref, ret_ref, out_ref, tend_ref, t2_ref):
    chunks = ret_ref.shape[1] // LANES
    tend_ref[...] = jnp.dot(back_ref[...], ret_ref[...], preferred_element_type=jnp.float32)

    def body(r2, carry):
        for h in range(chunks):
            lanes = pl.ds(h * LANES, LANES)
            t = tend_ref[pl.ds(pl.multiple_of(r2 * 16, 16), 16), lanes]
            t2_ref[h, pl.ds(0, 16, stride=2), :] = t
            t2_ref[h, pl.ds(1, 16, stride=2), :] = t
            spread = t2_ref[h]
            for half in range(2):
                row = 2 * r2 + half
                out_ref[row, :, lanes] = (
                    st_ref[row, :, lanes].astype(jnp.float32) + spread
                ).astype(out_ref.dtype)
        return carry

    lax.fori_loop(0, 16, body, 0)


def edge_kernel(cl_ref, cr_ref, top_ref, bot_ref, lsend_ref, rsend_ref):
    sub = lax.broadcasted_iota(jnp.int32, cl_ref.shape[1:], 0)
    for side_ref, out_ref, b, j in ((cr_ref, lsend_ref, 7, 3), (cl_ref, rsend_ref, 0, 0)):
        above = top_ref[j, pl.ds(b, 1), :]
        below = bot_ref[j, pl.ds(b, 1), :]
        first = side_ref[0] + jnp.where(sub == 0, above, pltpu.roll(side_ref[3], 1, 0))
        last = side_ref[3] + jnp.where(sub == 7, below, pltpu.roll(side_ref[0], 7, 0))
        out_ref[0] = first
        out_ref[1] = side_ref[1]
        out_ref[2] = side_ref[2]
        out_ref[3] = last


def run_edges(cl, cr, top, bot):
    return pl.pallas_call(
        edge_kernel,
        out_shape=[jax.ShapeDtypeStruct(cl.shape, cl.dtype)] * 2,
    )(cl, cr, top, bot)


def spec(shape, lane_axis=None):
    nd = len(shape)

    def index(h):
        return tuple(h if d == lane_axis else 0 for d in range(nd))

    return pl.BlockSpec(shape, index)


def run_section(tracers, coef):
    rows, cols, features = tracers.shape
    nb = features // LANES
    return pl.pallas_call(
        section_kernel,
        grid=(nb,),
        in_specs=[
            spec((rows, cols, LANES), 2),
            pl.BlockSpec((3, rows, cols, LANES), lambda h: (0, 0, 0, 0)),
        ],
        out_specs=[
            spec((4, 4, 8, 8, LANES), 4),
            spec((4, 8, LANES), 2),
            spec((4, 8, LANES), 2),
            spec((4, 8, LANES), 2),
            spec((4, 8, LANES), 2),
        ],
        out_shape=[
            jax.ShapeDtypeStruct((4, 4, 8, 8, features), jnp.float32),
            jax.ShapeDtypeStruct((4, 8, features), jnp.float32),
            jax.ShapeDtypeStruct((4, 8, features), jnp.float32),
            jax.ShapeDtypeStruct((4, 8, features), jnp.float32),
            jax.ShapeDtypeStruct((4, 8, features), jnp.float32),
        ],
        scratch_shapes=[pltpu.VMEM((rows, cols, LANES), jnp.float32)],
    )(tracers, coef)


def run_settle(w, top, bot, lax_halo, rax_halo, coef):
    features = w.shape[-1]
    nb = features // LANES
    return pl.pallas_call(
        settle_kernel,
        grid=(nb,),
        in_specs=[
            spec((4, 4, 8, 8, LANES), 4),
            spec((4, 8, LANES), 2),
            spec((4, 8, LANES), 2),
            spec((4, 8, LANES), 2),
            spec((4, 8, LANES), 2),
            pl.BlockSpec((2, 32, 32, LANES), lambda h: (1, 0, 0, 0)),
        ],
        out_specs=[
            spec((32, 32, LANES), 2),
            spec((256, LANES), 1),
        ],
        out_shape=[
            jax.ShapeDtypeStruct((32, 32, features), jnp.bfloat16),
            jax.ShapeDtypeStruct((256, features), jnp.bfloat16),
        ],
        scratch_shapes=[pltpu.VMEM((32, 32, LANES), jnp.float32)],
    )(w, top, bot, lax_halo, rax_halo, coef)


def run_finish(settled, back_table, returned):
    rows, cols, features = settled.shape
    width = 4 * LANES
    nb = features // width
    return pl.pallas_call(
        finish_kernel,
        grid=(nb,),
        in_specs=[
            spec((rows, cols, width), 2),
            spec(back_table.shape),
            spec((returned.shape[0], width), 1),
        ],
        out_specs=spec((rows, cols, width), 2),
        out_shape=jax.ShapeDtypeStruct(settled.shape, jnp.bfloat16),
        scratch_shapes=[
            pltpu.VMEM((back_table.shape[0], width), jnp.float32),
            pltpu.VMEM((width // LANES, cols, LANES), jnp.float32),
        ],
    )(settled, back_table, returned)


def shift(x, axis, step):
    count = lax.axis_size(axis)
    return lax.ppermute(x, axis, [(k, (k + step) % count) for k in range(count)])


def on_device(
    tracers, metric_x, metric_y, mass_weight, mass_inverse, phys_slot, diff_inverse, span_cost
):
    point_rows, point_cols, features = tracers.shape
    coef = jnp.broadcast_to(
        jnp.stack([metric_x, metric_y, mass_weight, mass_inverse])[..., None],
        (4, point_rows, point_cols, LANES),
    )

    w, rt, rb, cl, cr = run_section(tracers, coef)
    top = shift(rb, "elem", 1)
    bot = shift(rt, "elem", -1)

    lsend, rsend = run_edges(cl, cr, top, bot)
    lax_halo = shift(lsend, "sub", 1)
    rax_halo = shift(rsend, "sub", -1)
    settled, columns = run_settle(w, top, bot, lax_halo, rax_halo, coef)

    column_count = columns.shape[0]
    slot_k = phys_slot.reshape(8, 2, 8, 2).transpose(0, 1, 3, 2).reshape(-1)
    device_count = lax.axis_size(("elem", "sub"))
    capacity = max(1, 2 * column_count // device_count)
    slot_total = device_count * capacity
    target = slot_k // column_count
    landing = slot_k % column_count
    column_order = jnp.arange(column_count)
    earlier = (target[None, :] == target[:, None]) & (column_order[None, :] < column_order[:, None])
    position = jnp.sum(earlier.astype(jnp.int32), axis=1)
    dest_row = target * capacity + position
    slot_order = jnp.arange(slot_total)
    send_table = (slot_order[:, None] == dest_row[None, :]).astype(jnp.bfloat16)
    label_block = jnp.where(
        jnp.arange(LANES)[None, :] == 0, (landing + 1)[:, None].astype(jnp.bfloat16), 0
    ).astype(jnp.bfloat16)
    payload = jnp.concatenate([columns, label_block], axis=1)
    outgoing = jnp.einsum(
        "dck,kf->dcf", send_table.reshape(device_count, capacity, column_count), payload,
        preferred_element_type=jnp.float32,
    ).astype(jnp.bfloat16)
    arrived = lax.all_to_all(outgoing, ("elem", "sub"), split_axis=0, concat_axis=0, tiled=True)
    arrived = arrived.reshape(-1, features + LANES)
    arrived_labels = arrived[:, features].astype(jnp.int32) - 1
    place_table = (column_order[:, None] == arrived_labels[None, :]).astype(jnp.bfloat16)
    slot_state = jnp.dot(
        place_table, arrived[:, :features], preferred_element_type=jnp.float32
    ).astype(jnp.bfloat16)
    span_count = span_cost.shape[0]
    levels = diff_inverse.shape[1]
    start_state = slot_state.reshape(span_count, -1, levels)

    def substep(step_index, current):
        updated = jnp.einsum(
            "crm,clm->crl", current, diff_inverse, preferred_element_type=jnp.float32
        ).astype(jnp.bfloat16)
        return jnp.where((step_index < span_cost)[:, None, None], updated, current)

    final_state = lax.fori_loop(0, jnp.max(span_cost), substep, start_state)
    tendency = (
        (final_state.astype(jnp.float32) - start_state.astype(jnp.float32))
        .astype(jnp.bfloat16)
        .reshape(column_count, features)
    )
    reply_table = (arrived_labels[:, None] == column_order[None, :]).astype(jnp.bfloat16)
    replies = jnp.dot(reply_table, tendency, preferred_element_type=jnp.float32).astype(
        jnp.bfloat16
    )
    replies = replies.reshape(device_count, capacity, features)
    returned = lax.all_to_all(replies, ("elem", "sub"), split_axis=0, concat_axis=0, tiled=True)
    returned = returned.reshape(slot_total, features)
    dest_nat = dest_row.reshape(8, 2, 2, 8).transpose(0, 1, 3, 2).reshape(-1)
    back_table = (dest_nat[:, None] == slot_order[None, :]).astype(jnp.bfloat16)
    return run_finish(settled, back_table, returned)


def solution(mesh):
    in_specs = (
        P("elem", "sub", None),
        P("elem", "sub"),
        P("elem", "sub"),
        P("elem", "sub"),
        P("elem", "sub"),
        P(("elem", "sub")),
        P(("elem", "sub"), None, None),
        P(("elem", "sub")),
    )
    out_specs = P("elem", "sub", None)
    return jax.shard_map(
        on_device, mesh=mesh, in_specs=in_specs, out_specs=out_specs, check_vma=False
    )
```

```python
import math

import jax
import jax.numpy as jnp
import numpy as np
from jax import lax
from jax.experimental import pallas as pl
from jax.experimental.pallas import tpu as pltpu
from jax.sharding import PartitionSpec as P

diffusion_nu = 0.01
LANES = 128


def gll_matrix():
    gll_nodes = np.array([-1.0, -1.0 / math.sqrt(5.0), 1.0 / math.sqrt(5.0), 1.0])
    result = np.zeros((4, 4))
    for row_node in range(4):
        for col_node in range(4):
            if row_node == col_node:
                total = 0.0
                for other_node in range(4):
                    if other_node != row_node:
                        total += 1.0 / (gll_nodes[row_node] - gll_nodes[other_node])
                result[row_node, col_node] = total
            else:
                product_top = 1.0
                product_low = 1.0
                for other_node in range(4):
                    if other_node != col_node:
                        product_low *= gll_nodes[col_node] - gll_nodes[other_node]
                        if other_node != row_node:
                            product_top *= gll_nodes[row_node] - gll_nodes[other_node]
                result[row_node, col_node] = product_top / product_low
    return result


DERIV = [[float(np.float32(v)) for v in row] for row in gll_matrix()]


def mix(coefs, terms):
    total = coefs[0] * terms[0]
    for c, t in zip(coefs[1:], terms[1:]):
        total = total + c * t
    return total


def split_coefficients(coef_ref, cs_ref):
    @pl.when(pl.program_id(0) == 0)
    def _():
        def fill(a, carry):
            for kind in range(cs_ref.shape[0]):
                for i in range(4):
                    for j in range(4):
                        cs_ref[kind, i, j, a] = coef_ref[kind, 4 * a + i, pl.ds(j, 8, stride=4), :]
            return carry

        lax.fori_loop(0, 8, fill, 0)


def section_kernel(q_ref, coef_ref, w_ref, rt_ref, rb_ref, cl_ref, cr_ref, s_ref, cs_ref):
    split_coefficients(coef_ref, cs_ref)
    s_ref[...] = q_ref[...].astype(jnp.float32)
    d = DERIV

    def body(a, carry):
        q = [[s_ref[4 * a + i, pl.ds(j, 8, stride=4), :] for j in range(4)] for i in range(4)]
        mx, my, mw = (
            [[cs_ref[kind, i, j, a] for j in range(4)] for i in range(4)] for kind in range(3)
        )
        tx = [
            [mx[k][j] * mix(d[k], [q[m][j] for m in range(4)]) for j in range(4)]
            for k in range(4)
        ]
        ty = [
            [my[i][k] * mix(d[k], [q[i][m] for m in range(4)]) for k in range(4)]
            for i in range(4)
        ]
        for i in range(4):
            for j in range(4):
                wx = mix([d[k][i] for k in range(4)], [tx[k][j] for k in range(4)])
                wy = mix([d[k][j] for k in range(4)], [ty[i][k] for k in range(4)])
                w_ref[i, j, a] = mw[i][j] * (q[i][j] - diffusion_nu * (wx + wy))
        return carry

    lax.fori_loop(0, 8, body, 0)
    for j in range(4):
        rt_ref[j] = w_ref[0, j, 0]
        rb_ref[j] = w_ref[3, j, 7]
    for i in range(4):
        for a in range(8):
            cl_ref[i, pl.ds(a, 1), :] = w_ref[i, 0, a, pl.ds(0, 1), :]
            cr_ref[i, pl.ds(a, 1), :] = w_ref[i, 3, a, pl.ds(7, 1), :]


def settle_kernel(
    w_ref, top_ref, bot_ref, lax_ref, rax_ref, coef_ref, st_ref, col_ref, ss_ref, cs_ref
):
    split_coefficients(coef_ref, cs_ref)
    sub = lax.broadcasted_iota(jnp.int32, (8, LANES), 0)

    def body(a, carry):
        x = [[w_ref[i, j, a] for j in range(4)] for i in range(4)]
        mw = [[cs_ref[0, i, j, a] for j in range(4)] for i in range(4)]
        mi = [[cs_ref[1, i, j, a] for j in range(4)] for i in range(4)]
        up = [
            jnp.where(a == 0, top_ref[j], w_ref[3, j, jnp.maximum(a - 1, 0)]) for j in range(4)
        ]
        dn = [
            jnp.where(a == 7, bot_ref[j], w_ref[0, j, jnp.minimum(a + 1, 7)]) for j in range(4)
        ]
        ax = [
            [x[0][j] + up[j] for j in range(4)],
            x[1],
            x[2],
            [x[3][j] + dn[j] for j in range(4)],
        ]
        settled = [[None] * 4 for _ in range(4)]
        for i in range(4):
            left = lax_ref[i, pl.ds(a, 1), :]
            right = rax_ref[i, pl.ds(a, 1), :]
            prev3 = jnp.where(sub == 0, left, pltpu.roll(ax[i][3], 1, 0))
            next0 = jnp.where(sub == 7, right, pltpu.roll(ax[i][0], 7, 0))
            summed = [ax[i][0] + prev3, ax[i][1], ax[i][2], ax[i][3] + next0]
            for j in range(4):
                value = (mi[i][j] * summed[j]).astype(jnp.bfloat16)
                settled[i][j] = value.astype(jnp.float32)
                ss_ref[4 * a + i, pl.ds(j, 8, stride=4), :] = settled[i][j]
        for p in range(2):
            pair = []
            for q in range(2):
                num = None
                den = None
                for i in (2 * p, 2 * p + 1):
                    for j in (2 * q, 2 * q + 1):
                        term = mw[i][j] * settled[i][j]
                        num = term if num is None else num + term
                        den = mw[i][j] if den is None else den + mw[i][j]
                pair.append(num / den)
            row = pl.multiple_of((a * 2 + p) * 16, 16)
            col_ref[pl.ds(row, 16), :] = jnp.concatenate(pair, axis=0).astype(col_ref.dtype)
        return carry

    lax.fori_loop(0, 8, body, 0)
    st_ref[...] = ss_ref[...].astype(st_ref.dtype)


def finish_kernel(st_ref, back_ref, ret_ref, out_ref, tend_ref, t2_ref):
    chunks = ret_ref.shape[1] // LANES
    tend_ref[...] = jnp.dot(back_ref[...], ret_ref[...], preferred_element_type=jnp.float32)

    def body(r2, carry):
        for h in range(chunks):
            lanes = pl.ds(h * LANES, LANES)
            t = tend_ref[pl.ds(pl.multiple_of(r2 * 16, 16), 16), lanes]
            t2_ref[h, pl.ds(0, 16, stride=2), :] = t
            t2_ref[h, pl.ds(1, 16, stride=2), :] = t
            spread = t2_ref[h]
            for half in range(2):
                row = 2 * r2 + half
                out_ref[row, :, lanes] = (
                    st_ref[row, :, lanes].astype(jnp.float32) + spread
                ).astype(out_ref.dtype)
        return carry

    lax.fori_loop(0, 16, body, 0)


def edge_kernel(cl_ref, cr_ref, top_ref, bot_ref, lsend_ref, rsend_ref):
    sub = lax.broadcasted_iota(jnp.int32, cl_ref.shape[1:], 0)
    for side_ref, out_ref, b, j in ((cr_ref, lsend_ref, 7, 3), (cl_ref, rsend_ref, 0, 0)):
        above = top_ref[j, pl.ds(b, 1), :]
        below = bot_ref[j, pl.ds(b, 1), :]
        first = side_ref[0] + jnp.where(sub == 0, above, pltpu.roll(side_ref[3], 1, 0))
        last = side_ref[3] + jnp.where(sub == 7, below, pltpu.roll(side_ref[0], 7, 0))
        out_ref[0] = first
        out_ref[1] = side_ref[1]
        out_ref[2] = side_ref[2]
        out_ref[3] = last


def run_edges(cl, cr, top, bot):
    return pl.pallas_call(
        edge_kernel,
        out_shape=[jax.ShapeDtypeStruct(cl.shape, cl.dtype)] * 2,
    )(cl, cr, top, bot)


def spec(shape, lane_axis=None):
    nd = len(shape)

    def index(h):
        return tuple(h if d == lane_axis else 0 for d in range(nd))

    return pl.BlockSpec(shape, index)


def run_section(tracers, coef):
    rows, cols, features = tracers.shape
    nb = features // LANES
    return pl.pallas_call(
        section_kernel,
        grid=(nb,),
        in_specs=[
            spec((rows, cols, LANES), 2),
            pl.BlockSpec((3, rows, cols, LANES), lambda h: (0, 0, 0, 0)),
        ],
        out_specs=[
            spec((4, 4, 8, 8, LANES), 4),
            spec((4, 8, LANES), 2),
            spec((4, 8, LANES), 2),
            spec((4, 8, LANES), 2),
            spec((4, 8, LANES), 2),
        ],
        out_shape=[
            jax.ShapeDtypeStruct((4, 4, 8, 8, features), jnp.float32),
            jax.ShapeDtypeStruct((4, 8, features), jnp.float32),
            jax.ShapeDtypeStruct((4, 8, features), jnp.float32),
            jax.ShapeDtypeStruct((4, 8, features), jnp.float32),
            jax.ShapeDtypeStruct((4, 8, features), jnp.float32),
        ],
        scratch_shapes=[
            pltpu.VMEM((rows, cols, LANES), jnp.float32),
            pltpu.VMEM((3, 4, 4, 8, 8, LANES), jnp.float32),
        ],
        compiler_params=pltpu.CompilerParams(dimension_semantics=("arbitrary",)),
    )(tracers, coef)


def run_settle(w, top, bot, lax_halo, rax_halo, coef):
    features = w.shape[-1]
    nb = features // LANES
    return pl.pallas_call(
        settle_kernel,
        grid=(nb,),
        in_specs=[
            spec((4, 4, 8, 8, LANES), 4),
            spec((4, 8, LANES), 2),
            spec((4, 8, LANES), 2),
            spec((4, 8, LANES), 2),
            spec((4, 8, LANES), 2),
            pl.BlockSpec((2, 32, 32, LANES), lambda h: (1, 0, 0, 0)),
        ],
        out_specs=[
            spec((32, 32, LANES), 2),
            spec((256, LANES), 1),
        ],
        out_shape=[
            jax.ShapeDtypeStruct((32, 32, features), jnp.bfloat16),
            jax.ShapeDtypeStruct((256, features), jnp.bfloat16),
        ],
        scratch_shapes=[
            pltpu.VMEM((32, 32, LANES), jnp.float32),
            pltpu.VMEM((2, 4, 4, 8, 8, LANES), jnp.float32),
        ],
        compiler_params=pltpu.CompilerParams(dimension_semantics=("arbitrary",)),
    )(w, top, bot, lax_halo, rax_halo, coef)


def run_finish(settled, back_table, returned):
    rows, cols, features = settled.shape
    width = 4 * LANES
    nb = features // width
    return pl.pallas_call(
        finish_kernel,
        grid=(nb,),
        in_specs=[
            spec((rows, cols, width), 2),
            spec(back_table.shape),
            spec((returned.shape[0], width), 1),
        ],
        out_specs=spec((rows, cols, width), 2),
        out_shape=jax.ShapeDtypeStruct(settled.shape, jnp.bfloat16),
        scratch_shapes=[
            pltpu.VMEM((back_table.shape[0], width), jnp.float32),
            pltpu.VMEM((width // LANES, cols, LANES), jnp.float32),
        ],
    )(settled, back_table, returned)


def shift(x, axis, step):
    count = lax.axis_size(axis)
    return lax.ppermute(x, axis, [(k, (k + step) % count) for k in range(count)])


def on_device(
    tracers, metric_x, metric_y, mass_weight, mass_inverse, phys_slot, diff_inverse, span_cost
):
    point_rows, point_cols, features = tracers.shape
    coef = jnp.broadcast_to(
        jnp.stack([metric_x, metric_y, mass_weight, mass_inverse])[..., None],
        (4, point_rows, point_cols, LANES),
    )

    w, rt, rb, cl, cr = run_section(tracers, coef)
    top = shift(rb, "elem", 1)
    bot = shift(rt, "elem", -1)

    lsend, rsend = run_edges(cl, cr, top, bot)
    lax_halo = shift(lsend, "sub", 1)
    rax_halo = shift(rsend, "sub", -1)
    settled, columns = run_settle(w, top, bot, lax_halo, rax_halo, coef)

    column_count = columns.shape[0]
    slot_k = phys_slot.reshape(8, 2, 8, 2).transpose(0, 1, 3, 2).reshape(-1)
    device_count = lax.axis_size(("elem", "sub"))
    capacity = max(1, 2 * column_count // device_count)
    slot_total = device_count * capacity
    target = slot_k // column_count
    landing = slot_k % column_count
    column_order = jnp.arange(column_count)
    earlier = (target[None, :] == target[:, None]) & (column_order[None, :] < column_order[:, None])
    position = jnp.sum(earlier.astype(jnp.int32), axis=1)
    dest_row = target * capacity + position
    slot_order = jnp.arange(slot_total)
    send_table = (slot_order[:, None] == dest_row[None, :]).astype(jnp.bfloat16)
    label_block = jnp.where(
        jnp.arange(LANES)[None, :] == 0, (landing + 1)[:, None].astype(jnp.bfloat16), 0
    ).astype(jnp.bfloat16)
    payload = jnp.concatenate([columns, label_block], axis=1)
    outgoing = jnp.einsum(
        "dck,kf->dcf", send_table.reshape(device_count, capacity, column_count), payload,
        preferred_element_type=jnp.float32,
    ).astype(jnp.bfloat16)
    arrived = lax.all_to_all(outgoing, ("elem", "sub"), split_axis=0, concat_axis=0, tiled=True)
    arrived = arrived.reshape(-1, features + LANES)
    arrived_labels = arrived[:, features].astype(jnp.int32) - 1
    place_table = (column_order[:, None] == arrived_labels[None, :]).astype(jnp.bfloat16)
    slot_state = jnp.dot(
        place_table, arrived[:, :features], preferred_element_type=jnp.float32
    ).astype(jnp.bfloat16)
    span_count = span_cost.shape[0]
    levels = diff_inverse.shape[1]
    start_state = slot_state.reshape(span_count, -1, levels)

    def substep(step_index, current):
        updated = jnp.einsum(
            "crm,clm->crl", current, diff_inverse, preferred_element_type=jnp.float32
        ).astype(jnp.bfloat16)
        return jnp.where((step_index < span_cost)[:, None, None], updated, current)

    final_state = lax.fori_loop(0, jnp.max(span_cost), substep, start_state)
    tendency = (
        (final_state.astype(jnp.float32) - start_state.astype(jnp.float32))
        .astype(jnp.bfloat16)
        .reshape(column_count, features)
    )
    reply_table = (arrived_labels[:, None] == column_order[None, :]).astype(jnp.bfloat16)
    replies = jnp.dot(reply_table, tendency, preferred_element_type=jnp.float32).astype(
        jnp.bfloat16
    )
    replies = replies.reshape(device_count, capacity, features)
    returned = lax.all_to_all(replies, ("elem", "sub"), split_axis=0, concat_axis=0, tiled=True)
    returned = returned.reshape(slot_total, features)
    dest_nat = dest_row.reshape(8, 2, 2, 8).transpose(0, 1, 3, 2).reshape(-1)
    back_table = (dest_nat[:, None] == slot_order[None, :]).astype(jnp.bfloat16)
    return run_finish(settled, back_table, returned)


def solution(mesh):
    in_specs = (
        P("elem", "sub", None),
        P("elem", "sub"),
        P("elem", "sub"),
        P("elem", "sub"),
        P("elem", "sub"),
        P(("elem", "sub")),
        P(("elem", "sub"), None, None),
        P(("elem", "sub")),
    )
    out_specs = P("elem", "sub", None)
    return jax.shard_map(
        on_device, mesh=mesh, in_specs=in_specs, out_specs=out_specs, check_vma=False
    )
```

```python
import math

import jax
import jax.numpy as jnp
import numpy as np
from jax import lax
from jax.experimental import pallas as pl
from jax.experimental.pallas import tpu as pltpu
from jax.sharding import PartitionSpec as P

diffusion_nu = 0.01
LANES = 128


def gll_matrix():
    gll_nodes = np.array([-1.0, -1.0 / math.sqrt(5.0), 1.0 / math.sqrt(5.0), 1.0])
    result = np.zeros((4, 4))
    for row_node in range(4):
        for col_node in range(4):
            if row_node == col_node:
                total = 0.0
                for other_node in range(4):
                    if other_node != row_node:
                        total += 1.0 / (gll_nodes[row_node] - gll_nodes[other_node])
                result[row_node, col_node] = total
            else:
                product_top = 1.0
                product_low = 1.0
                for other_node in range(4):
                    if other_node != col_node:
                        product_low *= gll_nodes[col_node] - gll_nodes[other_node]
                        if other_node != row_node:
                            product_top *= gll_nodes[row_node] - gll_nodes[other_node]
                result[row_node, col_node] = product_top / product_low
    return result


DERIV = [[float(np.float32(v)) for v in row] for row in gll_matrix()]


def mix(coefs, terms):
    total = coefs[0] * terms[0]
    for c, t in zip(coefs[1:], terms[1:]):
        total = total + c * t
    return total


def interleave_matrix(dtype, inverse=False):
    c = lax.broadcasted_iota(jnp.int32, (32, 32), 0)
    k = lax.broadcasted_iota(jnp.int32, (32, 32), 1)
    if inverse:
        c, k = k, c
    return (k == (c % 4) * 8 + c // 4).astype(dtype)


def split_coefficients(coef_ref, cs_ref):
    @pl.when(pl.program_id(0) == 0)
    def _():
        def fill(a, carry):
            for kind in range(cs_ref.shape[0]):
                for i in range(4):
                    for j in range(4):
                        cs_ref[kind, i, j, a] = coef_ref[kind, 4 * a + i, pl.ds(j, 8, stride=4), :]
            return carry

        lax.fori_loop(0, 8, fill, 0)


def section_kernel(q_ref, coef_ref, w_ref, rt_ref, rb_ref, cl_ref, cr_ref, cs_ref):
    split_coefficients(coef_ref, cs_ref)
    d = DERIV
    split = interleave_matrix(q_ref.dtype, inverse=True)

    def body(a, carry):
        q = []
        for i in range(4):
            rows = jnp.dot(split, q_ref[4 * a + i], preferred_element_type=jnp.float32)
            q.append([rows[8 * j:8 * (j + 1)] for j in range(4)])
        mx, my, mw = (
            [[cs_ref[kind, i, j, a] for j in range(4)] for i in range(4)] for kind in range(3)
        )
        tx = [
            [mx[k][j] * mix(d[k], [q[m][j] for m in range(4)]) for j in range(4)]
            for k in range(4)
        ]
        ty = [
            [my[i][k] * mix(d[k], [q[i][m] for m in range(4)]) for k in range(4)]
            for i in range(4)
        ]
        for i in range(4):
            for j in range(4):
                wx = mix([d[k][i] for k in range(4)], [tx[k][j] for k in range(4)])
                wy = mix([d[k][j] for k in range(4)], [ty[i][k] for k in range(4)])
                w_ref[i, j, a] = mw[i][j] * (q[i][j] - diffusion_nu * (wx + wy))
        return carry

    lax.fori_loop(0, 8, body, 0)
    for j in range(4):
        rt_ref[j] = w_ref[0, j, 0]
        rb_ref[j] = w_ref[3, j, 7]
    for i in range(4):
        for a in range(8):
            cl_ref[i, pl.ds(a, 1), :] = w_ref[i, 0, a, pl.ds(0, 1), :]
            cr_ref[i, pl.ds(a, 1), :] = w_ref[i, 3, a, pl.ds(7, 1), :]


def settle_kernel(w_ref, top_ref, bot_ref, lax_ref, rax_ref, coef_ref, st_ref, col_ref, cs_ref):
    split_coefficients(coef_ref, cs_ref)
    sub = lax.broadcasted_iota(jnp.int32, (8, LANES), 0)
    merge = interleave_matrix(jnp.float32)

    def body(a, carry):
        x = [[w_ref[i, j, a] for j in range(4)] for i in range(4)]
        mw = [[cs_ref[0, i, j, a] for j in range(4)] for i in range(4)]
        mi = [[cs_ref[1, i, j, a] for j in range(4)] for i in range(4)]
        up = [
            jnp.where(a == 0, top_ref[j], w_ref[3, j, jnp.maximum(a - 1, 0)]) for j in range(4)
        ]
        dn = [
            jnp.where(a == 7, bot_ref[j], w_ref[0, j, jnp.minimum(a + 1, 7)]) for j in range(4)
        ]
        ax = [
            [x[0][j] + up[j] for j in range(4)],
            x[1],
            x[2],
            [x[3][j] + dn[j] for j in range(4)],
        ]
        settled = [[None] * 4 for _ in range(4)]
        for i in range(4):
            left = lax_ref[i, pl.ds(a, 1), :]
            right = rax_ref[i, pl.ds(a, 1), :]
            prev3 = jnp.where(sub == 0, left, pltpu.roll(ax[i][3], 1, 0))
            next0 = jnp.where(sub == 7, right, pltpu.roll(ax[i][0], 7, 0))
            summed = [ax[i][0] + prev3, ax[i][1], ax[i][2], ax[i][3] + next0]
            for j in range(4):
                value = (mi[i][j] * summed[j]).astype(jnp.bfloat16)
                settled[i][j] = value.astype(jnp.float32)
            natural = jnp.dot(
                merge, jnp.concatenate(settled[i], axis=0), preferred_element_type=jnp.float32
            )
            st_ref[4 * a + i] = natural.astype(st_ref.dtype)
        for p in range(2):
            pair = []
            for q in range(2):
                num = None
                den = None
                for i in (2 * p, 2 * p + 1):
                    for j in (2 * q, 2 * q + 1):
                        term = mw[i][j] * settled[i][j]
                        num = term if num is None else num + term
                        den = mw[i][j] if den is None else den + mw[i][j]
                pair.append(num / den)
            row = pl.multiple_of((a * 2 + p) * 16, 16)
            col_ref[pl.ds(row, 16), :] = jnp.concatenate(pair, axis=0).astype(col_ref.dtype)
        return carry

    lax.fori_loop(0, 8, body, 0)


def finish_kernel(st_ref, back_ref, ret_ref, out_ref, tend_ref, t2_ref):
    chunks = ret_ref.shape[1] // LANES
    tend_ref[...] = jnp.dot(back_ref[...], ret_ref[...], preferred_element_type=jnp.float32)

    def body(r2, carry):
        for h in range(chunks):
            lanes = pl.ds(h * LANES, LANES)
            t = tend_ref[pl.ds(pl.multiple_of(r2 * 16, 16), 16), lanes]
            t2_ref[h, pl.ds(0, 16, stride=2), :] = t
            t2_ref[h, pl.ds(1, 16, stride=2), :] = t
            spread = t2_ref[h]
            for half in range(2):
                row = 2 * r2 + half
                out_ref[row, :, lanes] = (
                    st_ref[row, :, lanes].astype(jnp.float32) + spread
                ).astype(out_ref.dtype)
        return carry

    lax.fori_loop(0, 16, body, 0)


def edge_kernel(cl_ref, cr_ref, top_ref, bot_ref, lsend_ref, rsend_ref):
    sub = lax.broadcasted_iota(jnp.int32, cl_ref.shape[1:], 0)
    for side_ref, out_ref, b, j in ((cr_ref, lsend_ref, 7, 3), (cl_ref, rsend_ref, 0, 0)):
        above = top_ref[j, pl.ds(b, 1), :]
        below = bot_ref[j, pl.ds(b, 1), :]
        first = side_ref[0] + jnp.where(sub == 0, above, pltpu.roll(side_ref[3], 1, 0))
        last = side_ref[3] + jnp.where(sub == 7, below, pltpu.roll(side_ref[0], 7, 0))
        out_ref[0] = first
        out_ref[1] = side_ref[1]
        out_ref[2] = side_ref[2]
        out_ref[3] = last


def run_edges(cl, cr, top, bot):
    return pl.pallas_call(
        edge_kernel,
        out_shape=[jax.ShapeDtypeStruct(cl.shape, cl.dtype)] * 2,
    )(cl, cr, top, bot)


def spec(shape, lane_axis=None):
    nd = len(shape)

    def index(h):
        return tuple(h if d == lane_axis else 0 for d in range(nd))

    return pl.BlockSpec(shape, index)


def run_section(tracers, coef):
    rows, cols, features = tracers.shape
    nb = features // LANES
    return pl.pallas_call(
        section_kernel,
        grid=(nb,),
        in_specs=[
            spec((rows, cols, LANES), 2),
            pl.BlockSpec((3, rows, cols, LANES), lambda h: (0, 0, 0, 0)),
        ],
        out_specs=[
            spec((4, 4, 8, 8, LANES), 4),
            spec((4, 8, LANES), 2),
            spec((4, 8, LANES), 2),
            spec((4, 8, LANES), 2),
            spec((4, 8, LANES), 2),
        ],
        out_shape=[
            jax.ShapeDtypeStruct((4, 4, 8, 8, features), jnp.float32),
            jax.ShapeDtypeStruct((4, 8, features), jnp.float32),
            jax.ShapeDtypeStruct((4, 8, features), jnp.float32),
            jax.ShapeDtypeStruct((4, 8, features), jnp.float32),
            jax.ShapeDtypeStruct((4, 8, features), jnp.float32),
        ],
        scratch_shapes=[pltpu.VMEM((3, 4, 4, 8, 8, LANES), jnp.float32)],
        compiler_params=pltpu.CompilerParams(dimension_semantics=("arbitrary",)),
    )(tracers, coef)


def run_settle(w, top, bot, lax_halo, rax_halo, coef):
    features = w.shape[-1]
    nb = features // LANES
    return pl.pallas_call(
        settle_kernel,
        grid=(nb,),
        in_specs=[
            spec((4, 4, 8, 8, LANES), 4),
            spec((4, 8, LANES), 2),
            spec((4, 8, LANES), 2),
            spec((4, 8, LANES), 2),
            spec((4, 8, LANES), 2),
            pl.BlockSpec((2, 32, 32, LANES), lambda h: (1, 0, 0, 0)),
        ],
        out_specs=[
            spec((32, 32, LANES), 2),
            spec((256, LANES), 1),
        ],
        out_shape=[
            jax.ShapeDtypeStruct((32, 32, features), jnp.bfloat16),
            jax.ShapeDtypeStruct((256, features), jnp.bfloat16),
        ],
        scratch_shapes=[pltpu.VMEM((2, 4, 4, 8, 8, LANES), jnp.float32)],
        compiler_params=pltpu.CompilerParams(dimension_semantics=("arbitrary",)),
    )(w, top, bot, lax_halo, rax_halo, coef)


def run_finish(settled, back_table, returned):
    rows, cols, features = settled.shape
    width = 4 * LANES
    nb = features // width
    return pl.pallas_call(
        finish_kernel,
        grid=(nb,),
        in_specs=[
            spec((rows, cols, width), 2),
            spec(back_table.shape),
            spec((returned.shape[0], width), 1),
        ],
        out_specs=spec((rows, cols, width), 2),
        out_shape=jax.ShapeDtypeStruct(settled.shape, jnp.bfloat16),
        scratch_shapes=[
            pltpu.VMEM((back_table.shape[0], width), jnp.float32),
            pltpu.VMEM((width // LANES, cols, LANES), jnp.float32),
        ],
    )(settled, back_table, returned)


def shift(x, axis, step):
    count = lax.axis_size(axis)
    return lax.ppermute(x, axis, [(k, (k + step) % count) for k in range(count)])


def on_device(
    tracers, metric_x, metric_y, mass_weight, mass_inverse, phys_slot, diff_inverse, span_cost
):
    point_rows, point_cols, features = tracers.shape
    coef = jnp.broadcast_to(
        jnp.stack([metric_x, metric_y, mass_weight, mass_inverse])[..., None],
        (4, point_rows, point_cols, LANES),
    )

    w, rt, rb, cl, cr = run_section(tracers, coef)
    top = shift(rb, "elem", 1)
    bot = shift(rt, "elem", -1)

    lsend, rsend = run_edges(cl, cr, top, bot)
    lax_halo = shift(lsend, "sub", 1)
    rax_halo = shift(rsend, "sub", -1)
    settled, columns = run_settle(w, top, bot, lax_halo, rax_halo, coef)

    column_count = columns.shape[0]
    slot_k = phys_slot.reshape(8, 2, 8, 2).transpose(0, 1, 3, 2).reshape(-1)
    device_count = lax.axis_size(("elem", "sub"))
    capacity = max(1, 2 * column_count // device_count)
    slot_total = device_count * capacity
    target = slot_k // column_count
    landing = slot_k % column_count
    column_order = jnp.arange(column_count)
    earlier = (target[None, :] == target[:, None]) & (column_order[None, :] < column_order[:, None])
    position = jnp.sum(earlier.astype(jnp.int32), axis=1)
    dest_row = target * capacity + position
    slot_order = jnp.arange(slot_total)
    send_table = (slot_order[:, None] == dest_row[None, :]).astype(jnp.bfloat16)
    label_block = jnp.where(
        jnp.arange(LANES)[None, :] == 0, (landing + 1)[:, None].astype(jnp.bfloat16), 0
    ).astype(jnp.bfloat16)
    payload = jnp.concatenate([columns, label_block], axis=1)
    outgoing = jnp.einsum(
        "dck,kf->dcf", send_table.reshape(device_count, capacity, column_count), payload,
        preferred_element_type=jnp.float32,
    ).astype(jnp.bfloat16)
    arrived = lax.all_to_all(outgoing, ("elem", "sub"), split_axis=0, concat_axis=0, tiled=True)
    arrived = arrived.reshape(-1, features + LANES)
    arrived_labels = arrived[:, features].astype(jnp.int32) - 1
    place_table = (column_order[:, None] == arrived_labels[None, :]).astype(jnp.bfloat16)
    slot_state = jnp.dot(
        place_table, arrived[:, :features], preferred_element_type=jnp.float32
    ).astype(jnp.bfloat16)
    span_count = span_cost.shape[0]
    levels = diff_inverse.shape[1]
    start_state = slot_state.reshape(span_count, -1, levels)

    def substep(step_index, current):
        updated = jnp.einsum(
            "crm,clm->crl", current, diff_inverse, preferred_element_type=jnp.float32
        ).astype(jnp.bfloat16)
        return jnp.where((step_index < span_cost)[:, None, None], updated, current)

    final_state = lax.fori_loop(0, jnp.max(span_cost), substep, start_state)
    tendency = (
        (final_state.astype(jnp.float32) - start_state.astype(jnp.float32))
        .astype(jnp.bfloat16)
        .reshape(column_count, features)
    )
    reply_table = (arrived_labels[:, None] == column_order[None, :]).astype(jnp.bfloat16)
    replies = jnp.dot(reply_table, tendency, preferred_element_type=jnp.float32).astype(
        jnp.bfloat16
    )
    replies = replies.reshape(device_count, capacity, features)
    returned = lax.all_to_all(replies, ("elem", "sub"), split_axis=0, concat_axis=0, tiled=True)
    returned = returned.reshape(slot_total, features)
    dest_nat = dest_row.reshape(8, 2, 2, 8).transpose(0, 1, 3, 2).reshape(-1)
    back_table = (dest_nat[:, None] == slot_order[None, :]).astype(jnp.bfloat16)
    return run_finish(settled, back_table, returned)


def solution(mesh):
    in_specs = (
        P("elem", "sub", None),
        P("elem", "sub"),
        P("elem", "sub"),
        P("elem", "sub"),
        P("elem", "sub"),
        P(("elem", "sub")),
        P(("elem", "sub"), None, None),
        P(("elem", "sub")),
    )
    out_specs = P("elem", "sub", None)
    return jax.shard_map(
        on_device, mesh=mesh, in_specs=in_specs, out_specs=out_specs, check_vma=False
    )
```

```python
import math

import jax
import jax.numpy as jnp
import numpy as np
from jax import lax
from jax.experimental import pallas as pl
from jax.experimental.pallas import tpu as pltpu
from jax.sharding import PartitionSpec as P

diffusion_nu = 0.01
LANES = 128


def gll_matrix():
    gll_nodes = np.array([-1.0, -1.0 / math.sqrt(5.0), 1.0 / math.sqrt(5.0), 1.0])
    result = np.zeros((4, 4))
    for row_node in range(4):
        for col_node in range(4):
            if row_node == col_node:
                total = 0.0
                for other_node in range(4):
                    if other_node != row_node:
                        total += 1.0 / (gll_nodes[row_node] - gll_nodes[other_node])
                result[row_node, col_node] = total
            else:
                product_top = 1.0
                product_low = 1.0
                for other_node in range(4):
                    if other_node != col_node:
                        product_low *= gll_nodes[col_node] - gll_nodes[other_node]
                        if other_node != row_node:
                            product_top *= gll_nodes[row_node] - gll_nodes[other_node]
                result[row_node, col_node] = product_top / product_low
    return result


DERIV = [[float(np.float32(v)) for v in row] for row in gll_matrix()]


def split_operator(matrix):
    table = []
    for i in range(2):
        row = matrix[i]
        table.append(tuple(float(np.float32(v)) for v in (
            (row[0] + row[3]) / 2, (row[1] + row[2]) / 2, (row[0] - row[3]) / 2, (row[1] - row[2]) / 2
        )))
    return table


GLL = gll_matrix()
SLOPE = split_operator(GLL)
WEAK = split_operator(diffusion_nu * GLL.T)


def apply_split(table, t):
    e0, d0 = t[0] + t[3], t[0] - t[3]
    e1, d1 = t[1] + t[2], t[1] - t[2]
    out = [None] * 4
    for i, (ae, be, ad, bd) in enumerate(table):
        even = ae * e0 + be * e1
        odd = ad * d0 + bd * d1
        out[i] = even + odd
        out[3 - i] = odd - even
    return out


def mix(coefs, terms):
    total = coefs[0] * terms[0]
    for c, t in zip(coefs[1:], terms[1:]):
        total = total + c * t
    return total


def split_coefficients(coef_ref, cs_ref):
    @pl.when(pl.program_id(0) == 0)
    def _():
        def fill(a, carry):
            for kind in range(cs_ref.shape[0]):
                for i in range(4):
                    for j in range(4):
                        cs_ref[kind, i, j, a] = coef_ref[kind, 4 * a + i, pl.ds(j, 8, stride=4), :]
            return carry

        lax.fori_loop(0, 8, fill, 0)


def section_kernel(q_ref, coef_ref, w_ref, rt_ref, rb_ref, cl_ref, cr_ref, s_ref, cs_ref):
    split_coefficients(coef_ref, cs_ref)
    s_ref[...] = q_ref[...].astype(jnp.float32)
    d = DERIV

    def body(a, carry):
        q = [[s_ref[4 * a + i, pl.ds(j, 8, stride=4), :] for j in range(4)] for i in range(4)]
        mx, my, mw = (
            [[cs_ref[kind, i, j, a] for j in range(4)] for i in range(4)] for kind in range(3)
        )
        sx = [apply_split(SLOPE, [q[m][j] for m in range(4)]) for j in range(4)]
        tx = [[mx[k][j] * sx[j][k] for k in range(4)] for j in range(4)]
        wx = [apply_split(WEAK, tx[j]) for j in range(4)]
        sy = [apply_split(SLOPE, q[i]) for i in range(4)]
        ty = [[my[i][k] * sy[i][k] for k in range(4)] for i in range(4)]
        wy = [apply_split(WEAK, ty[i]) for i in range(4)]
        for i in range(4):
            for j in range(4):
                w_ref[i, j, a] = mw[i][j] * (q[i][j] - (wx[j][i] + wy[i][j]))
        return carry

    lax.fori_loop(0, 8, body, 0)
    for j in range(4):
        rt_ref[j] = w_ref[0, j, 0]
        rb_ref[j] = w_ref[3, j, 7]
    for i in range(4):
        for a in range(8):
            cl_ref[i, pl.ds(a, 1), :] = w_ref[i, 0, a, pl.ds(0, 1), :]
            cr_ref[i, pl.ds(a, 1), :] = w_ref[i, 3, a, pl.ds(7, 1), :]


def settle_kernel(
    w_ref, top_ref, bot_ref, lax_ref, rax_ref, coef_ref, st_ref, col_ref, ss_ref, cs_ref
):
    split_coefficients(coef_ref, cs_ref)
    sub = lax.broadcasted_iota(jnp.int32, (8, LANES), 0)

    def body(a, carry):
        x = [[w_ref[i, j, a] for j in range(4)] for i in range(4)]
        mw = [[cs_ref[0, i, j, a] for j in range(4)] for i in range(4)]
        mi = [[cs_ref[1, i, j, a] for j in range(4)] for i in range(4)]
        up = [
            jnp.where(a == 0, top_ref[j], w_ref[3, j, jnp.maximum(a - 1, 0)]) for j in range(4)
        ]
        dn = [
            jnp.where(a == 7, bot_ref[j], w_ref[0, j, jnp.minimum(a + 1, 7)]) for j in range(4)
        ]
        ax = [
            [x[0][j] + up[j] for j in range(4)],
            x[1],
            x[2],
            [x[3][j] + dn[j] for j in range(4)],
        ]
        settled = [[None] * 4 for _ in range(4)]
        for i in range(4):
            left = lax_ref[i, pl.ds(a, 1), :]
            right = rax_ref[i, pl.ds(a, 1), :]
            prev3 = jnp.where(sub == 0, left, pltpu.roll(ax[i][3], 1, 0))
            next0 = jnp.where(sub == 7, right, pltpu.roll(ax[i][0], 7, 0))
            summed = [ax[i][0] + prev3, ax[i][1], ax[i][2], ax[i][3] + next0]
            for j in range(4):
                value = (mi[i][j] * summed[j]).astype(jnp.bfloat16)
                settled[i][j] = value.astype(jnp.float32)
                ss_ref[4 * a + i, pl.ds(j, 8, stride=4), :] = settled[i][j]
        for p in range(2):
            pair = []
            for q in range(2):
                num = None
                den = None
                for i in (2 * p, 2 * p + 1):
                    for j in (2 * q, 2 * q + 1):
                        term = mw[i][j] * settled[i][j]
                        num = term if num is None else num + term
                        den = mw[i][j] if den is None else den + mw[i][j]
                pair.append(num / den)
            row = pl.multiple_of((a * 2 + p) * 16, 16)
            col_ref[pl.ds(row, 16), :] = jnp.concatenate(pair, axis=0).astype(col_ref.dtype)
        return carry

    lax.fori_loop(0, 8, body, 0)
    st_ref[...] = ss_ref[...].astype(st_ref.dtype)


def finish_kernel(st_ref, back_ref, ret_ref, out_ref, tend_ref, t2_ref):
    chunks = ret_ref.shape[1] // LANES
    tend_ref[...] = jnp.dot(back_ref[...], ret_ref[...], preferred_element_type=jnp.float32)

    def body(r2, carry):
        for h in range(chunks):
            lanes = pl.ds(h * LANES, LANES)
            t = tend_ref[pl.ds(pl.multiple_of(r2 * 16, 16), 16), lanes]
            t2_ref[h, pl.ds(0, 16, stride=2), :] = t
            t2_ref[h, pl.ds(1, 16, stride=2), :] = t
            spread = t2_ref[h]
            for half in range(2):
                row = 2 * r2 + half
                out_ref[row, :, lanes] = (
                    st_ref[row, :, lanes].astype(jnp.float32) + spread
                ).astype(out_ref.dtype)
        return carry

    lax.fori_loop(0, 16, body, 0)


def edge_kernel(cl_ref, cr_ref, top_ref, bot_ref, lsend_ref, rsend_ref):
    sub = lax.broadcasted_iota(jnp.int32, cl_ref.shape[1:], 0)
    for side_ref, out_ref, b, j in ((cr_ref, lsend_ref, 7, 3), (cl_ref, rsend_ref, 0, 0)):
        above = top_ref[j, pl.ds(b, 1), :]
        below = bot_ref[j, pl.ds(b, 1), :]
        first = side_ref[0] + jnp.where(sub == 0, above, pltpu.roll(side_ref[3], 1, 0))
        last = side_ref[3] + jnp.where(sub == 7, below, pltpu.roll(side_ref[0], 7, 0))
        out_ref[0] = first
        out_ref[1] = side_ref[1]
        out_ref[2] = side_ref[2]
        out_ref[3] = last


def run_edges(cl, cr, top, bot):
    return pl.pallas_call(
        edge_kernel,
        out_shape=[jax.ShapeDtypeStruct(cl.shape, cl.dtype)] * 2,
    )(cl, cr, top, bot)


def spec(shape, lane_axis=None):
    nd = len(shape)

    def index(h):
        return tuple(h if d == lane_axis else 0 for d in range(nd))

    return pl.BlockSpec(shape, index)


def run_section(tracers, coef):
    rows, cols, features = tracers.shape
    nb = features // LANES
    return pl.pallas_call(
        section_kernel,
        grid=(nb,),
        in_specs=[
            spec((rows, cols, LANES), 2),
            pl.BlockSpec((3, rows, cols, LANES), lambda h: (0, 0, 0, 0)),
        ],
        out_specs=[
            spec((4, 4, 8, 8, LANES), 4),
            spec((4, 8, LANES), 2),
            spec((4, 8, LANES), 2),
            spec((4, 8, LANES), 2),
            spec((4, 8, LANES), 2),
        ],
        out_shape=[
            jax.ShapeDtypeStruct((4, 4, 8, 8, features), jnp.float32),
            jax.ShapeDtypeStruct((4, 8, features), jnp.float32),
            jax.ShapeDtypeStruct((4, 8, features), jnp.float32),
            jax.ShapeDtypeStruct((4, 8, features), jnp.float32),
            jax.ShapeDtypeStruct((4, 8, features), jnp.float32),
        ],
        scratch_shapes=[
            pltpu.VMEM((rows, cols, LANES), jnp.float32),
            pltpu.VMEM((3, 4, 4, 8, 8, LANES), jnp.float32),
        ],
        compiler_params=pltpu.CompilerParams(dimension_semantics=("arbitrary",)),
    )(tracers, coef)


def run_settle(w, top, bot, lax_halo, rax_halo, coef):
    features = w.shape[-1]
    nb = features // LANES
    return pl.pallas_call(
        settle_kernel,
        grid=(nb,),
        in_specs=[
            spec((4, 4, 8, 8, LANES), 4),
            spec((4, 8, LANES), 2),
            spec((4, 8, LANES), 2),
            spec((4, 8, LANES), 2),
            spec((4, 8, LANES), 2),
            pl.BlockSpec((2, 32, 32, LANES), lambda h: (1, 0, 0, 0)),
        ],
        out_specs=[
            spec((32, 32, LANES), 2),
            spec((256, LANES), 1),
        ],
        out_shape=[
            jax.ShapeDtypeStruct((32, 32, features), jnp.bfloat16),
            jax.ShapeDtypeStruct((256, features), jnp.bfloat16),
        ],
        scratch_shapes=[
            pltpu.VMEM((32, 32, LANES), jnp.float32),
            pltpu.VMEM((2, 4, 4, 8, 8, LANES), jnp.float32),
        ],
        compiler_params=pltpu.CompilerParams(dimension_semantics=("arbitrary",)),
    )(w, top, bot, lax_halo, rax_halo, coef)


def run_finish(settled, back_table, returned):
    rows, cols, features = settled.shape
    width = 4 * LANES
    nb = features // width
    return pl.pallas_call(
        finish_kernel,
        grid=(nb,),
        in_specs=[
            spec((rows, cols, width), 2),
            spec(back_table.shape),
            spec((returned.shape[0], width), 1),
        ],
        out_specs=spec((rows, cols, width), 2),
        out_shape=jax.ShapeDtypeStruct(settled.shape, jnp.bfloat16),
        scratch_shapes=[
            pltpu.VMEM((back_table.shape[0], width), jnp.float32),
            pltpu.VMEM((width // LANES, cols, LANES), jnp.float32),
        ],
    )(settled, back_table, returned)


def shift(x, axis, step):
    count = lax.axis_size(axis)
    return lax.ppermute(x, axis, [(k, (k + step) % count) for k in range(count)])


def on_device(
    tracers, metric_x, metric_y, mass_weight, mass_inverse, phys_slot, diff_inverse, span_cost
):
    point_rows, point_cols, features = tracers.shape
    coef = jnp.broadcast_to(
        jnp.stack([metric_x, metric_y, mass_weight, mass_inverse])[..., None],
        (4, point_rows, point_cols, LANES),
    )

    w, rt, rb, cl, cr = run_section(tracers, coef)
    top = shift(rb, "elem", 1)
    bot = shift(rt, "elem", -1)

    lsend, rsend = run_edges(cl, cr, top, bot)
    lax_halo = shift(lsend, "sub", 1)
    rax_halo = shift(rsend, "sub", -1)
    settled, columns = run_settle(w, top, bot, lax_halo, rax_halo, coef)

    column_count = columns.shape[0]
    slot_k = phys_slot.reshape(8, 2, 8, 2).transpose(0, 1, 3, 2).reshape(-1)
    device_count = lax.axis_size(("elem", "sub"))
    capacity = max(1, 2 * column_count // device_count)
    slot_total = device_count * capacity
    target = slot_k // column_count
    landing = slot_k % column_count
    column_order = jnp.arange(column_count)
    earlier = (target[None, :] == target[:, None]) & (column_order[None, :] < column_order[:, None])
    position = jnp.sum(earlier.astype(jnp.int32), axis=1)
    dest_row = target * capacity + position
    slot_order = jnp.arange(slot_total)
    send_table = (slot_order[:, None] == dest_row[None, :]).astype(jnp.bfloat16)
    label_block = jnp.where(
        jnp.arange(LANES)[None, :] == 0, (landing + 1)[:, None].astype(jnp.bfloat16), 0
    ).astype(jnp.bfloat16)
    payload = jnp.concatenate([columns, label_block], axis=1)
    outgoing = jnp.einsum(
        "dck,kf->dcf", send_table.reshape(device_count, capacity, column_count), payload,
        preferred_element_type=jnp.float32,
    ).astype(jnp.bfloat16)
    arrived = lax.all_to_all(outgoing, ("elem", "sub"), split_axis=0, concat_axis=0, tiled=True)
    arrived = arrived.reshape(-1, features + LANES)
    arrived_labels = arrived[:, features].astype(jnp.int32) - 1
    place_table = (column_order[:, None] == arrived_labels[None, :]).astype(jnp.bfloat16)
    slot_state = jnp.dot(
        place_table, arrived[:, :features], preferred_element_type=jnp.float32
    ).astype(jnp.bfloat16)
    span_count = span_cost.shape[0]
    levels = diff_inverse.shape[1]
    start_state = slot_state.reshape(span_count, -1, levels)

    def substep(step_index, current):
        updated = jnp.einsum(
            "crm,clm->crl", current, diff_inverse, preferred_element_type=jnp.float32
        ).astype(jnp.bfloat16)
        return jnp.where((step_index < span_cost)[:, None, None], updated, current)

    final_state = lax.fori_loop(0, jnp.max(span_cost), substep, start_state)
    tendency = (
        (final_state.astype(jnp.float32) - start_state.astype(jnp.float32))
        .astype(jnp.bfloat16)
        .reshape(column_count, features)
    )
    reply_table = (arrived_labels[:, None] == column_order[None, :]).astype(jnp.bfloat16)
    replies = jnp.dot(reply_table, tendency, preferred_element_type=jnp.float32).astype(
        jnp.bfloat16
    )
    replies = replies.reshape(device_count, capacity, features)
    returned = lax.all_to_all(replies, ("elem", "sub"), split_axis=0, concat_axis=0, tiled=True)
    returned = returned.reshape(slot_total, features)
    dest_nat = dest_row.reshape(8, 2, 2, 8).transpose(0, 1, 3, 2).reshape(-1)
    back_table = (dest_nat[:, None] == slot_order[None, :]).astype(jnp.bfloat16)
    return run_finish(settled, back_table, returned)


def solution(mesh):
    in_specs = (
        P("elem", "sub", None),
        P("elem", "sub"),
        P("elem", "sub"),
        P("elem", "sub"),
        P("elem", "sub"),
        P(("elem", "sub")),
        P(("elem", "sub"), None, None),
        P(("elem", "sub")),
    )
    out_specs = P("elem", "sub", None)
    return jax.shard_map(
        on_device, mesh=mesh, in_specs=in_specs, out_specs=out_specs, check_vma=False
    )
```

```python
import math

import jax
import jax.numpy as jnp
import numpy as np
from jax import lax
from jax.experimental import pallas as pl
from jax.experimental.pallas import tpu as pltpu
from jax.sharding import PartitionSpec as P

diffusion_nu = 0.01
LANES = 128


def gll_matrix():
    gll_nodes = np.array([-1.0, -1.0 / math.sqrt(5.0), 1.0 / math.sqrt(5.0), 1.0])
    result = np.zeros((4, 4))
    for row_node in range(4):
        for col_node in range(4):
            if row_node == col_node:
                total = 0.0
                for other_node in range(4):
                    if other_node != row_node:
                        total += 1.0 / (gll_nodes[row_node] - gll_nodes[other_node])
                result[row_node, col_node] = total
            else:
                product_top = 1.0
                product_low = 1.0
                for other_node in range(4):
                    if other_node != col_node:
                        product_low *= gll_nodes[col_node] - gll_nodes[other_node]
                        if other_node != row_node:
                            product_top *= gll_nodes[row_node] - gll_nodes[other_node]
                result[row_node, col_node] = product_top / product_low
    return result


DERIV = [[float(np.float32(v)) for v in row] for row in gll_matrix()]


def split_operator(matrix):
    table = []
    for i in range(2):
        row = matrix[i]
        table.append(tuple(float(np.float32(v)) for v in (
            (row[0] + row[3]) / 2, (row[1] + row[2]) / 2, (row[0] - row[3]) / 2, (row[1] - row[2]) / 2
        )))
    return table


GLL = gll_matrix()
SLOPE = split_operator(GLL)
WEAK = split_operator(diffusion_nu * GLL.T)


def apply_split(table, t):
    e0, d0 = t[0] + t[3], t[0] - t[3]
    e1, d1 = t[1] + t[2], t[1] - t[2]
    out = [None] * 4
    for i, (ae, be, ad, bd) in enumerate(table):
        even = ae * e0 + be * e1
        odd = ad * d0 + bd * d1
        out[i] = even + odd
        out[3 - i] = odd - even
    return out


def mix(coefs, terms):
    total = coefs[0] * terms[0]
    for c, t in zip(coefs[1:], terms[1:]):
        total = total + c * t
    return total


def section_kernel(q_ref, coef_ref, w_ref, rt_ref, rb_ref, cl_ref, cr_ref, s_ref):
    s_ref[...] = q_ref[...].astype(jnp.float32)
    d = DERIV

    def body(a, carry):
        q = [[s_ref[4 * a + i, pl.ds(j, 8, stride=4), :] for j in range(4)] for i in range(4)]
        mx, my, mw = (
            [[coef_ref[kind, 4 * a + i, pl.ds(j, 8, stride=4), :] for j in range(4)]
             for i in range(4)]
            for kind in range(3)
        )
        sx = [apply_split(SLOPE, [q[m][j] for m in range(4)]) for j in range(4)]
        tx = [[mx[k][j] * sx[j][k] for k in range(4)] for j in range(4)]
        wx = [apply_split(WEAK, tx[j]) for j in range(4)]
        sy = [apply_split(SLOPE, q[i]) for i in range(4)]
        ty = [[my[i][k] * sy[i][k] for k in range(4)] for i in range(4)]
        wy = [apply_split(WEAK, ty[i]) for i in range(4)]
        for i in range(4):
            for j in range(4):
                w_ref[i, j, a] = mw[i][j] * (q[i][j] - (wx[j][i] + wy[i][j]))
        return carry

    lax.fori_loop(0, 8, body, 0)
    for j in range(4):
        rt_ref[j] = w_ref[0, j, 0]
        rb_ref[j] = w_ref[3, j, 7]
    for i in range(4):
        for a in range(8):
            cl_ref[i, pl.ds(a, 1), :] = w_ref[i, 0, a, pl.ds(0, 1), :]
            cr_ref[i, pl.ds(a, 1), :] = w_ref[i, 3, a, pl.ds(7, 1), :]


def settle_kernel(w_ref, top_ref, bot_ref, lax_ref, rax_ref, coef_ref, st_ref, col_ref, ss_ref):
    sub = lax.broadcasted_iota(jnp.int32, (8, LANES), 0)

    def body(a, carry):
        x = [[w_ref[i, j, a] for j in range(4)] for i in range(4)]
        mw = [[coef_ref[0, 4 * a + i, pl.ds(j, 8, stride=4), :] for j in range(4)] for i in range(4)]
        mi = [[coef_ref[1, 4 * a + i, pl.ds(j, 8, stride=4), :] for j in range(4)] for i in range(4)]
        up = [
            jnp.where(a == 0, top_ref[j], w_ref[3, j, jnp.maximum(a - 1, 0)]) for j in range(4)
        ]
        dn = [
            jnp.where(a == 7, bot_ref[j], w_ref[0, j, jnp.minimum(a + 1, 7)]) for j in range(4)
        ]
        ax = [
            [x[0][j] + up[j] for j in range(4)],
            x[1],
            x[2],
            [x[3][j] + dn[j] for j in range(4)],
        ]
        settled = [[None] * 4 for _ in range(4)]
        for i in range(4):
            left = lax_ref[i, pl.ds(a, 1), :]
            right = rax_ref[i, pl.ds(a, 1), :]
            prev3 = jnp.where(sub == 0, left, pltpu.roll(ax[i][3], 1, 0))
            next0 = jnp.where(sub == 7, right, pltpu.roll(ax[i][0], 7, 0))
            summed = [ax[i][0] + prev3, ax[i][1], ax[i][2], ax[i][3] + next0]
            for j in range(4):
                value = (mi[i][j] * summed[j]).astype(jnp.bfloat16)
                settled[i][j] = value.astype(jnp.float32)
                ss_ref[4 * a + i, pl.ds(j, 8, stride=4), :] = settled[i][j]
        for p in range(2):
            pair = []
            for q in range(2):
                num = None
                den = None
                for i in (2 * p, 2 * p + 1):
                    for j in (2 * q, 2 * q + 1):
                        term = mw[i][j] * settled[i][j]
                        num = term if num is None else num + term
                        den = mw[i][j] if den is None else den + mw[i][j]
                pair.append(num / den)
            row = pl.multiple_of((a * 2 + p) * 16, 16)
            col_ref[pl.ds(row, 16), :] = jnp.concatenate(pair, axis=0).astype(col_ref.dtype)
        return carry

    lax.fori_loop(0, 8, body, 0)
    st_ref[...] = ss_ref[...].astype(st_ref.dtype)


def finish_kernel(st_ref, tend_ref, out_ref, t2_ref):
    chunks = tend_ref.shape[1] // LANES

    def body(r2, carry):
        for h in range(chunks):
            lanes = pl.ds(h * LANES, LANES)
            t = tend_ref[pl.ds(pl.multiple_of(r2 * 16, 16), 16), lanes]
            t2_ref[h, pl.ds(0, 16, stride=2), :] = t
            t2_ref[h, pl.ds(1, 16, stride=2), :] = t
            spread = t2_ref[h]
            for half in range(2):
                row = 2 * r2 + half
                out_ref[row, :, lanes] = (
                    st_ref[row, :, lanes].astype(jnp.float32) + spread
                ).astype(out_ref.dtype)
        return carry

    lax.fori_loop(0, 16, body, 0)


def spec(shape, lane_axis=None):
    nd = len(shape)

    def index(h):
        return tuple(h if d == lane_axis else 0 for d in range(nd))

    return pl.BlockSpec(shape, index)


def run_section(tracers, coef):
    rows, cols, features = tracers.shape
    nb = features // LANES
    return pl.pallas_call(
        section_kernel,
        grid=(nb,),
        in_specs=[
            spec((rows, cols, LANES), 2),
            pl.BlockSpec((3, rows, cols, LANES), lambda h: (0, 0, 0, 0)),
        ],
        out_specs=[
            spec((4, 4, 8, 8, LANES), 4),
            spec((4, 8, LANES), 2),
            spec((4, 8, LANES), 2),
            spec((4, 8, LANES), 2),
            spec((4, 8, LANES), 2),
        ],
        out_shape=[
            jax.ShapeDtypeStruct((4, 4, 8, 8, features), jnp.float32),
            jax.ShapeDtypeStruct((4, 8, features), jnp.float32),
            jax.ShapeDtypeStruct((4, 8, features), jnp.float32),
            jax.ShapeDtypeStruct((4, 8, features), jnp.float32),
            jax.ShapeDtypeStruct((4, 8, features), jnp.float32),
        ],
        scratch_shapes=[pltpu.VMEM((rows, cols, LANES), jnp.float32)],
    )(tracers, coef)


def run_settle(w, top, bot, lax_halo, rax_halo, coef):
    features = w.shape[-1]
    nb = features // LANES
    return pl.pallas_call(
        settle_kernel,
        grid=(nb,),
        in_specs=[
            spec((4, 4, 8, 8, LANES), 4),
            spec((4, 8, LANES), 2),
            spec((4, 8, LANES), 2),
            spec((4, 8, LANES), 2),
            spec((4, 8, LANES), 2),
            pl.BlockSpec((2, 32, 32, LANES), lambda h: (1, 0, 0, 0)),
        ],
        out_specs=[
            spec((32, 32, LANES), 2),
            spec((256, LANES), 1),
        ],
        out_shape=[
            jax.ShapeDtypeStruct((32, 32, features), jnp.bfloat16),
            jax.ShapeDtypeStruct((256, features), jnp.bfloat16),
        ],
        scratch_shapes=[pltpu.VMEM((32, 32, LANES), jnp.float32)],
    )(w, top, bot, lax_halo, rax_halo, coef)


def run_finish(settled, tend):
    rows, cols, features = settled.shape
    width = 4 * LANES
    nb = features // width
    return pl.pallas_call(
        finish_kernel,
        grid=(nb,),
        in_specs=[spec((rows, cols, width), 2), spec((tend.shape[0], width), 1)],
        out_specs=spec((rows, cols, width), 2),
        out_shape=jax.ShapeDtypeStruct(settled.shape, jnp.bfloat16),
        scratch_shapes=[pltpu.VMEM((width // LANES, cols, LANES), jnp.float32)],
    )(settled, tend)


def shift(x, axis, step):
    count = lax.axis_size(axis)
    return lax.ppermute(x, axis, [(k, (k + step) % count) for k in range(count)])


def on_device(
    tracers, metric_x, metric_y, mass_weight, mass_inverse, phys_slot, diff_inverse, span_cost
):
    point_rows, point_cols, features = tracers.shape
    coef = jnp.broadcast_to(
        jnp.stack([metric_x, metric_y, mass_weight, mass_inverse])[..., None],
        (4, point_rows, point_cols, LANES),
    )

    w, rt, rb, cl, cr = run_section(tracers, coef)
    top = shift(rb, "elem", 1)
    bot = shift(rt, "elem", -1)

    def along_x(side, above, below):
        first = side[0] + jnp.concatenate([above[None], side[3, :-1]], axis=0)
        last = side[3] + jnp.concatenate([side[0, 1:], below[None]], axis=0)
        return jnp.stack([first, side[1], side[2], last])

    lax_halo = shift(along_x(cr, top[3, 7], bot[3, 7]), "sub", 1)
    rax_halo = shift(along_x(cl, top[0, 0], bot[0, 0]), "sub", -1)
    settled, columns = run_settle(w, top, bot, lax_halo, rax_halo, coef)

    column_count = columns.shape[0]
    slot_k = phys_slot.reshape(8, 2, 8, 2).transpose(0, 1, 3, 2).reshape(-1)
    device_count = lax.axis_size(("elem", "sub"))
    capacity = max(1, 2 * column_count // device_count)
    slot_total = device_count * capacity
    target = slot_k // column_count
    landing = slot_k % column_count
    column_order = jnp.arange(column_count)
    earlier = (target[None, :] == target[:, None]) & (column_order[None, :] < column_order[:, None])
    position = jnp.sum(earlier.astype(jnp.int32), axis=1)
    dest_row = target * capacity + position
    slot_order = jnp.arange(slot_total)
    send_table = (slot_order[:, None] == dest_row[None, :]).astype(jnp.bfloat16)
    label_block = jnp.where(
        jnp.arange(LANES)[None, :] == 0, (landing + 1)[:, None].astype(jnp.bfloat16), 0
    ).astype(jnp.bfloat16)
    payload = jnp.concatenate([columns, label_block], axis=1)
    outgoing = jnp.dot(send_table, payload, preferred_element_type=jnp.float32).astype(jnp.bfloat16)
    outgoing = outgoing.reshape(device_count, capacity, features + LANES)
    arrived = lax.all_to_all(outgoing, ("elem", "sub"), split_axis=0, concat_axis=0, tiled=True)
    arrived = arrived.reshape(-1, features + LANES)
    arrived_labels = arrived[:, features].astype(jnp.int32) - 1
    arrived = arrived[:, :features]
    place_table = (column_order[:, None] == arrived_labels[None, :]).astype(jnp.bfloat16)
    slot_state = jnp.dot(place_table, arrived, preferred_element_type=jnp.float32).astype(
        jnp.bfloat16
    )
    span_count = span_cost.shape[0]
    levels = diff_inverse.shape[1]
    start_state = slot_state.reshape(span_count, -1, levels)

    def substep(step_index, current):
        updated = jnp.einsum(
            "crm,clm->crl", current, diff_inverse, preferred_element_type=jnp.float32
        ).astype(jnp.bfloat16)
        return jnp.where((step_index < span_cost)[:, None, None], updated, current)

    final_state = lax.fori_loop(0, jnp.max(span_cost), substep, start_state)
    tendency = (
        (final_state.astype(jnp.float32) - start_state.astype(jnp.float32))
        .astype(jnp.bfloat16)
        .reshape(column_count, features)
    )
    reply_table = (arrived_labels[:, None] == column_order[None, :]).astype(jnp.bfloat16)
    replies = jnp.dot(reply_table, tendency, preferred_element_type=jnp.float32).astype(
        jnp.bfloat16
    )
    replies = replies.reshape(device_count, capacity, features)
    returned = lax.all_to_all(replies, ("elem", "sub"), split_axis=0, concat_axis=0, tiled=True)
    returned = returned.reshape(slot_total, features)
    dest_nat = dest_row.reshape(8, 2, 2, 8).transpose(0, 1, 3, 2).reshape(-1)
    back_table = (dest_nat[:, None] == slot_order[None, :]).astype(jnp.bfloat16)
    tend_cols = jnp.dot(back_table, returned, preferred_element_type=jnp.float32)
    return run_finish(settled, tend_cols)


def solution(mesh):
    in_specs = (
        P("elem", "sub", None),
        P("elem", "sub"),
        P("elem", "sub"),
        P("elem", "sub"),
        P("elem", "sub"),
        P(("elem", "sub")),
        P(("elem", "sub"), None, None),
        P(("elem", "sub")),
    )
    out_specs = P("elem", "sub", None)
    return jax.shard_map(
        on_device, mesh=mesh, in_specs=in_specs, out_specs=out_specs, check_vma=False
    )
```
